128 devices in a mesh: req: 16 (over z, y), seq: 8 (over x, core).
Axes of the slice: x: 4, y: 4, z: 4, core: 2. Of those that a mesh axis runs over, the one named last changes fastest.
Arguments:
- queries: bfloat16 [32, 48, 8192], P('req', None, 'seq')
- draft_key_value: bfloat16 [32, 48, 2048], P('req', None, 'seq'), may hold values from -6 to 6
- kv_cache: bfloat16 [32, 16384, 2048], P('req', 'seq')
- cache_lengths: int32 [32], P('req'), may hold values from 2 to 16384, as said below
- ancestors: int32 [32, 48, 48], P('req'), may hold values from 0 to 1, as said below
- dealing: int32 [32], replicated, may hold values from 0 to 31, as said below
- accepted_path: int32 [32, 8], P('req'), may hold values from 0 to 47
Outputs:
- verified_context: bfloat16 [1536, 8192], P(('req', 'seq'))
- kept_entries: bfloat16 [32, 8, 2048], P('req', None, 'seq')
The draws below stay inside these ranges and needn't reach their ends.
Inputs may be any that keep to these rules, and one draw needn't show every extreme that they name: `dealing`: a permutation of the request ids. `cache_lengths`: at least 2 live positions; some slot's cache is full (16384). Each row is the 0/1 indicator of a draft token's ancestors in its tree, the token itself included; token 0 is the root, a token's parent has a lower index.
All inputs are finite; a program needn't handle non-finite values.
Results may differ from the reference program's by a relative error of at most 0.0046.
Values may be sent and summed in bfloat16 or wider, within the bound.
No kernel may reach another device: no remote copies, remote signals or barrier semaphores. Data moves between devices by JAX's collectives and lax.ppermute only.
A program may use at most 128 MiB of HBM per device.

```python
import jax
import jax.numpy as jnp
from jax import lax

D = 8192
QUERY_HEADS = 64
KEY_HEADS = 8
HEAD_WIDTH = 128
TREE_TOKENS = 48
DEPTH = 8
BLK = 1024
REQUEST_COUNT = 32
CONTEXT_LENGTH = 16384


def dealing_order(key):
    return jax.random.permutation(jax.random.fold_in(key, 11), REQUEST_COUNT).astype(jnp.int32)


def front_rows(key):
    starting_rows = jax.random.normal(jax.random.fold_in(key, 12), (REQUEST_COUNT, KEY_HEADS, 2, HEAD_WIDTH), jnp.float32)
    additional_rows = jax.random.normal(jax.random.fold_in(key, 13), (REQUEST_COUNT, KEY_HEADS, 2, HEAD_WIDTH), jnp.float32)
    mixing = jnp.array([0.99, 0.0], jnp.float32)[:, None]
    fresh = jnp.array([0.1, 1.0], jnp.float32)[:, None]
    next_row_index = starting_rows * mixing + additional_rows * fresh
    return jnp.stack([starting_rows, next_row_index], axis=1).reshape(REQUEST_COUNT, 2, KEY_HEADS * 2 * HEAD_WIDTH)


def draw_kv_cache(key, part):
    complete_cache = jax.random.normal(jax.random.fold_in(key, 14), (REQUEST_COUNT, CONTEXT_LENGTH, KEY_HEADS * 2 * HEAD_WIDTH), jnp.float32)
    complete_cache = complete_cache.at[:, 0:2, :].set(front_rows(key))
    return complete_cache.astype(jnp.bfloat16)


def draw_queries(key, part):
    base_query = jax.random.normal(jax.random.fold_in(key, 15), (REQUEST_COUNT, TREE_TOKENS, QUERY_HEADS, HEAD_WIDTH), jnp.float32)
    return base_query.reshape(REQUEST_COUNT, TREE_TOKENS, QUERY_HEADS * HEAD_WIDTH).astype(jnp.bfloat16)


def draw_dealing(key, part):
    return dealing_order(key)


def draw_cache_lengths(key, part):
    lengths_drawn = jax.random.randint(jax.random.fold_in(key, 16), (REQUEST_COUNT,), 2, CONTEXT_LENGTH + 1, jnp.int32)
    picked = jax.random.randint(jax.random.fold_in(key, 17), (), 0, REQUEST_COUNT, jnp.int32)
    return lengths_drawn.at[picked].set(CONTEXT_LENGTH)


def draw_ancestors(key, part):
    raw_bits = jax.random.randint(jax.random.fold_in(key, 18), (REQUEST_COUNT, TREE_TOKENS), 0, 1 << 20, jnp.int32)
    closure = jnp.broadcast_to(jnp.eye(TREE_TOKENS, dtype=jnp.int32)[None], (REQUEST_COUNT, TREE_TOKENS, TREE_TOKENS))
    for node in range(1, TREE_TOKENS):
        parent = raw_bits[:, node] % node
        inherited = closure[jnp.arange(REQUEST_COUNT), parent]
        closure = closure.at[:, node].set(jnp.maximum(inherited, closure[:, node]))
    return closure


def place_ends(values, own_key, low, largest):
    shape = values.shape
    spot = [jax.random.randint(jax.random.fold_in(own_key, axis), (), 0, shape[axis]) for axis in range(len(shape))]
    values = values.at[tuple(spot)].set(low)
    longest = shape.index(max(shape))
    spot[longest] = (spot[longest] + 1) % shape[longest]
    return values.at[tuple(spot)].set(largest)


def level_of(own_key, extent, cuts, least, high):
    loudness, own = 1.0, jax.random.fold_in(own_key, 6)
    for dim, parts in cuts:
        draws = jnp.exp(jax.random.uniform(jax.random.fold_in(own, dim), (parts,), jnp.float32, least / len(cuts), high / len(cuts)))
        loudness = loudness * jnp.repeat(draws, extent[dim] // parts).reshape([-1 if axis == dim else 1 for axis in range(len(extent))])
    return loudness


def bell_draw(key, shape, spread, bound, split=(), held_as=jnp.bfloat16):
    entries = spread * jax.random.normal(key, shape, jnp.float32)
    if split:
        entries = entries * level_of(key, shape, split, -0.22, 0.18)
    return jnp.clip(entries, -bound, bound).astype(held_as)


def setup_inputs(seed: int = 0) -> dict:
    key_list = jax.random.split(jax.random.key(seed), 8)
    queries = draw_queries(jax.random.fold_in(key_list[7], 71), 0)
    draft_key_value = bell_draw(key_list[1], (REQUEST_COUNT, TREE_TOKENS, KEY_HEADS * 2 * HEAD_WIDTH), 1.0, 6.0, ((0, 16), (2, 8)))
    kv_cache = draw_kv_cache(jax.random.fold_in(key_list[7], 71), 0)
    cache_lengths = draw_cache_lengths(jax.random.fold_in(key_list[7], 71), 0)
    ancestors = draw_ancestors(jax.random.fold_in(key_list[7], 71), 0)
    dealing = draw_dealing(jax.random.fold_in(key_list[7], 71), 0)
    accepted_path = place_ends(jax.random.randint(key_list[6], (REQUEST_COUNT, DEPTH), 0, TREE_TOKENS), jax.random.fold_in(key_list[6], 1), 0, TREE_TOKENS - 1).astype(jnp.int32)
    return {"queries": queries, "draft_key_value": draft_key_value, "kv_cache": kv_cache, "cache_lengths": cache_lengths, "ancestors": ancestors, "dealing": dealing, "accepted_path": accepted_path}


def online_merge(earlier, later):
    max_a, sum_a, acc_a = earlier
    max_b, sum_b, acc_b = later
    row_max = jnp.maximum(max_a, max_b)
    scale_a = jnp.exp(max_a - row_max)
    scale_b = jnp.exp(max_b - row_max)
    return (row_max, sum_a * scale_a + sum_b * scale_b, acc_a * scale_a[..., None] + acc_b * scale_b[..., None])


def block_terms(grouped, key_rows, values, allowed):
    scores = jnp.einsum("tkgd,skd->kgts", grouped.astype(jnp.float32), key_rows.astype(jnp.float32)) * (HEAD_WIDTH ** -0.5)
    scores = jnp.where(allowed, scores, jnp.float32(-1e30))
    row_max = jnp.max(scores, axis=-1)
    weights = jnp.where(allowed, jnp.exp(scores - row_max[..., None]), jnp.float32(0.0))
    row_sum = jnp.sum(weights, axis=-1)
    rounded = weights.astype(jnp.bfloat16).astype(jnp.float32)
    row_acc = jnp.einsum("kgts,skd->kgtd", rounded, values.astype(jnp.float32))
    return row_max, row_sum, row_acc


def attend(query_rows, cache_rows, draft_rows, length, pos_offset, tree_mask, use_draft, blk_size):
    tree_len = query_rows.shape[0]
    kv_heads = cache_rows.shape[1] // (2 * HEAD_WIDTH)
    groups = query_rows.shape[1] // (HEAD_WIDTH * kv_heads)
    grouped = query_rows.reshape(tree_len, kv_heads, groups, HEAD_WIDTH)
    draft_part = draft_rows.reshape(tree_len, kv_heads, 2, HEAD_WIDTH)
    draft_allowed = jnp.logical_and(tree_mask > 0, use_draft)[None, None]
    running = block_terms(grouped, draft_part[:, :, 0], draft_part[:, :, 1], draft_allowed)
    blk_count = cache_rows.shape[0] // blk_size

    def body_step(blk_index, state):
        blk_start = blk_index * blk_size

        def absorb(state_in):
            cache_piece = lax.dynamic_slice_in_dim(cache_rows, blk_start, blk_size, 0).reshape(blk_size, kv_heads, 2, HEAD_WIDTH)
            positions = pos_offset + blk_start + jnp.arange(blk_size, dtype=jnp.int32)
            allowed = (positions < length)[None, None, None, :]
            return online_merge(state_in, block_terms(grouped, cache_piece[:, :, 0], cache_piece[:, :, 1], allowed))

        return lax.cond(pos_offset + blk_start < length, absorb, lambda state_in: state_in, state)

    return lax.fori_loop(0, blk_count, body_step, running)


def reference(queries, draft_key_value, kv_cache, cache_lengths, ancestors, dealing, accepted_path):
    expanded = jnp.broadcast_to(accepted_path[:, :, None], accepted_path.shape + (draft_key_value.shape[2],))
    kept_entries = jnp.take_along_axis(draft_key_value, expanded, axis=1)

    def one_request(slot_index):
        request = dealing[slot_index]
        row_max, row_sum, row_acc = attend(queries[request], kv_cache[slot_index], draft_key_value[request], cache_lengths[slot_index], 0, ancestors[slot_index], True, BLK)
        normed = (row_acc / row_sum[..., None]).transpose(2, 0, 1, 3).reshape(TREE_TOKENS, QUERY_HEADS * HEAD_WIDTH)
        return normed.astype(jnp.bfloat16)

    context = lax.map(one_request, jnp.arange(REQUEST_COUNT, dtype=jnp.int32))
    return context.reshape(REQUEST_COUNT * TREE_TOKENS, D), kept_entries
```

```python
import functools

import jax
import jax.numpy as jnp
from jax import lax
from jax.experimental import pallas as pl
from jax.experimental.pallas import tpu as pltpu
from jax.sharding import PartitionSpec as P

HEAD_WIDTH = 128
BLK = 1024
NEG = -1e30


def attn_kernel(live_ref, q_ref, kv_ref, m_ref, l_ref, acc_ref, *, n_blk, scale):
    slot = pl.program_id(0)
    live = live_ref[slot]
    q = q_ref[...]
    run_m = run_l = run_acc = None
    for b in range(n_blk):
        keys = kv_ref[b * BLK:(b + 1) * BLK, 0:HEAD_WIDTH]
        vals = kv_ref[b * BLK:(b + 1) * BLK, HEAD_WIDTH:2 * HEAD_WIDTH]
        s = lax.dot_general(
            q, keys, (((1,), (1,)), ((), ())), preferred_element_type=jnp.float32
        ) * scale
        pos = b * BLK + lax.broadcasted_iota(jnp.int32, (1, BLK), 1)
        allowed = pos < live
        s = jnp.where(allowed, s, jnp.float32(NEG))
        mb = jnp.max(s, axis=1, keepdims=True)
        w = jnp.where(allowed, jnp.exp(s - mb), jnp.float32(0.0))
        lb = jnp.sum(w, axis=1, keepdims=True)
        ob = jnp.dot(w.astype(jnp.bfloat16), vals, preferred_element_type=jnp.float32)
        if run_m is None:
            run_m, run_l, run_acc = mb, lb, ob
        else:
            new_m = jnp.maximum(run_m, mb)
            fa = jnp.exp(run_m - new_m)
            fb = jnp.exp(mb - new_m)
            run_l = run_l * fa + lb * fb
            run_acc = run_acc * fa + ob * fb
            run_m = new_m
    parts = m_ref.shape[0]
    rows = q.shape[0] // parts
    m_ref[...] = run_m.reshape(parts, rows, 1)
    l_ref[...] = run_l.reshape(parts, rows, 1)
    acc_ref[...] = run_acc.reshape(parts, rows, HEAD_WIDTH)


def local_attention(q4, kv, live, seq_count):
    slots, kvh, rows, _ = q4.shape
    positions = kv.shape[1]
    per_slot = seq_count // slots
    sub = rows // per_slot
    kern = functools.partial(attn_kernel, n_blk=positions // BLK, scale=HEAD_WIDTH ** (-0.5))
    grid_spec = pltpu.PrefetchScalarGridSpec(
        num_scalar_prefetch=1,
        grid=(slots, kvh),
        in_specs=[
            pl.BlockSpec((None, None, rows, HEAD_WIDTH), lambda i, k, lv: (i, k, 0, 0)),
            pl.BlockSpec((None, positions, 2 * HEAD_WIDTH), lambda i, k, lv: (i, 0, k)),
        ],
        out_specs=[
            pl.BlockSpec((per_slot, None, sub, 1), lambda i, k, lv: (i, k, 0, 0)),
            pl.BlockSpec((per_slot, None, sub, 1), lambda i, k, lv: (i, k, 0, 0)),
            pl.BlockSpec((per_slot, None, sub, HEAD_WIDTH), lambda i, k, lv: (i, k, 0, 0)),
        ],
    )
    return pl.pallas_call(
        kern,
        grid_spec=grid_spec,
        out_shape=[
            jax.ShapeDtypeStruct((seq_count, kvh, sub, 1), jnp.float32),
            jax.ShapeDtypeStruct((seq_count, kvh, sub, 1), jnp.float32),
            jax.ShapeDtypeStruct((seq_count, kvh, sub, HEAD_WIDTH), jnp.float32),
        ],
        compiler_params=pltpu.CompilerParams(
            dimension_semantics=("arbitrary", "arbitrary"),
            vmem_limit_bytes=48 * 1024 * 1024,
        ),
    )(live, q4, kv)


def body(queries, draft_key_value, kv_cache, cache_lengths, ancestors, dealing, accepted_path):
    local_reqs = kv_cache.shape[0]
    tree_len = queries.shape[1]
    picker = (
        accepted_path[:, :, None] == jnp.arange(tree_len, dtype=jnp.int32)[None, None, :]
    ).astype(jnp.bfloat16)
    kept_entries = jnp.einsum(
        "rit,rtc->ric", picker, draft_key_value, preferred_element_type=jnp.float32
    ).astype(jnp.bfloat16)
    every_query, every_draft = (
        lax.all_gather(queries, "req", axis=0, tiled=True),
        lax.all_gather(draft_key_value, "req", axis=0, tiled=True),
    )
    chosen = lax.dynamic_slice_in_dim(dealing, lax.axis_index("req") * local_reqs, local_reqs)
    own_query = jnp.stack(
        [
            lax.dynamic_index_in_dim(every_query, chosen[slot], 0, keepdims=False)
            for slot in range(local_reqs)
        ],
        axis=0,
    )
    own_draft = jnp.stack(
        [
            lax.dynamic_index_in_dim(every_draft, chosen[slot], 0, keepdims=False)
            for slot in range(local_reqs)
        ],
        axis=0,
    )
    seq_count = lax.axis_size("seq")
    full_query, full_draft = (
        lax.all_gather(own_query, "seq", axis=2, tiled=True),
        lax.all_gather(own_draft, "seq", axis=2, tiled=True),
    )
    position = lax.axis_index("seq")
    positions = kv_cache.shape[1]
    kv_heads = kv_cache.shape[2] // (2 * HEAD_WIDTH)
    groups = full_query.shape[2] // (HEAD_WIDTH * kv_heads)
    rows = tree_len * groups

    q4 = (
        full_query.reshape(local_reqs, tree_len, kv_heads, groups, HEAD_WIDTH)
        .transpose(0, 2, 1, 3, 4)
        .reshape(local_reqs, kv_heads, rows, HEAD_WIDTH)
    )
    live = jnp.clip(cache_lengths - position * positions, 0, positions).astype(jnp.int32)
    part_m, part_l, part_acc = local_attention(q4, kv_cache, live, seq_count)
    recv_m = lax.all_to_all(part_m, "seq", 0, 0, tiled=True)
    recv_l = lax.all_to_all(part_l, "seq", 0, 0, tiled=True)
    recv_acc = lax.all_to_all(part_acc, "seq", 0, 0, tiled=True)

    per_slot = seq_count // local_reqs
    tok = tree_len // per_slot
    my_slot = position // per_slot
    my_tok0 = (position % per_slot) * tok
    q_slot = lax.dynamic_index_in_dim(full_query, my_slot, 0, keepdims=False)
    q_mine = lax.dynamic_slice_in_dim(q_slot, my_tok0, tok, 0).reshape(
        tok, kv_heads, groups, HEAD_WIDTH
    )
    d_slot = lax.dynamic_index_in_dim(full_draft, my_slot, 0, keepdims=False).reshape(
        tree_len, kv_heads, 2, HEAD_WIDTH
    )
    anc = lax.dynamic_index_in_dim(ancestors, my_slot, 0, keepdims=False)
    anc = lax.dynamic_slice_in_dim(anc, my_tok0, tok, 0)
    allowed = (anc > 0)[None, :, None, :]
    sd = jnp.einsum(
        "tkgd,jkd->ktgj", q_mine, d_slot[:, :, 0], preferred_element_type=jnp.float32
    ) * HEAD_WIDTH ** (-0.5)
    sd = jnp.where(allowed, sd, jnp.float32(NEG))
    md = jnp.max(sd, axis=-1)
    wd = jnp.where(allowed, jnp.exp(sd - md[..., None]), jnp.float32(0.0))
    ld = jnp.sum(wd, axis=-1)
    od = jnp.einsum(
        "ktgj,jkd->ktgd", wd.astype(jnp.bfloat16), d_slot[:, :, 1], preferred_element_type=jnp.float32
    )
    md = md.reshape(kv_heads, tok * groups)
    ld = ld.reshape(kv_heads, tok * groups)
    od = od.reshape(kv_heads, tok * groups, HEAD_WIDTH)

    rm = recv_m[..., 0]
    rl = recv_l[..., 0]
    top = jnp.maximum(jnp.max(rm, axis=0), md)
    fr = jnp.exp(rm - top[None])
    fd = jnp.exp(md - top)
    den = jnp.sum(fr * rl, axis=0) + fd * ld
    num = jnp.sum(fr[..., None] * recv_acc, axis=0) + fd[..., None] * od
    res = num / den[..., None]
    context = (
        res.reshape(kv_heads, tok, groups, HEAD_WIDTH)
        .transpose(1, 0, 2, 3)
        .reshape(tok, kv_heads * groups * HEAD_WIDTH)
        .astype(jnp.bfloat16)
    )
    return (context, kept_entries)


def solution(mesh):
    placed = (
        P("req", None, "seq"),
        P("req", None, "seq"),
        P("req", "seq", None),
        P("req"),
        P("req", None, None),
        P(),
        P("req", None),
    )
    return jax.shard_map(
        body,
        mesh=mesh,
        in_specs=placed,
        out_specs=(P(("req", "seq"), None), P("req", None, "seq")),
        check_vma=False,
    )
```

```python
import functools

import jax
import jax.numpy as jnp
from jax import lax
from jax.experimental import pallas as pl
from jax.experimental.pallas import tpu as pltpu
from jax.sharding import PartitionSpec as P

HEAD_WIDTH = 128
BLK = 1024
NEG = -1e30


def attn_kernel(live_ref, q_ref, kv_ref, m_ref, l_ref, acc_ref, *, n_blk, scale):
    slot = pl.program_id(0)
    live = live_ref[slot]
    q = q_ref[...]
    run_m = run_l = run_acc = None
    for b in range(n_blk):
        keys = kv_ref[b * BLK:(b + 1) * BLK, 0:HEAD_WIDTH]
        vals = kv_ref[b * BLK:(b + 1) * BLK, HEAD_WIDTH:2 * HEAD_WIDTH]
        s = lax.dot_general(
            q, keys, (((1,), (1,)), ((), ())), preferred_element_type=jnp.float32
        ) * scale
        pos = b * BLK + lax.broadcasted_iota(jnp.int32, (1, BLK), 1)
        allowed = pos < live
        s = jnp.where(allowed, s, jnp.float32(NEG))
        mb = jnp.max(s, axis=1, keepdims=True)
        w = jnp.where(allowed, jnp.exp(s - mb), jnp.float32(0.0))
        lb = jnp.sum(w, axis=1, keepdims=True)
        ob = jnp.dot(w.astype(jnp.bfloat16), vals, preferred_element_type=jnp.float32)
        if run_m is None:
            run_m, run_l, run_acc = mb, lb, ob
        else:
            new_m = jnp.maximum(run_m, mb)
            fa = jnp.exp(run_m - new_m)
            fb = jnp.exp(mb - new_m)
            run_l = run_l * fa + lb * fb
            run_acc = run_acc * fa + ob * fb
            run_m = new_m
    parts = m_ref.shape[0]
    rows = q.shape[0] // parts
    m_ref[...] = run_m.reshape(parts, rows, 1)
    l_ref[...] = run_l.reshape(parts, rows, 1)
    acc_ref[...] = run_acc.reshape(parts, rows, HEAD_WIDTH)


def local_attention(q4, kv, live, seq_count):
    slots, kvh, rows, _ = q4.shape
    positions = kv.shape[1]
    per_slot = seq_count // slots
    sub = rows // per_slot
    kern = functools.partial(attn_kernel, n_blk=positions // BLK, scale=HEAD_WIDTH ** (-0.5))
    grid_spec = pltpu.PrefetchScalarGridSpec(
        num_scalar_prefetch=1,
        grid=(slots, kvh),
        in_specs=[
            pl.BlockSpec((None, None, rows, HEAD_WIDTH), lambda i, k, lv: (i, k, 0, 0)),
            pl.BlockSpec((None, positions, 2 * HEAD_WIDTH), lambda i, k, lv: (i, 0, k)),
        ],
        out_specs=[
            pl.BlockSpec((per_slot, None, sub, 1), lambda i, k, lv: (i, k, 0, 0)),
            pl.BlockSpec((per_slot, None, sub, 1), lambda i, k, lv: (i, k, 0, 0)),
            pl.BlockSpec((per_slot, None, sub, HEAD_WIDTH), lambda i, k, lv: (i, k, 0, 0)),
        ],
    )
    return pl.pallas_call(
        kern,
        grid_spec=grid_spec,
        out_shape=[
            jax.ShapeDtypeStruct((seq_count, kvh, sub, 1), jnp.float32),
            jax.ShapeDtypeStruct((seq_count, kvh, sub, 1), jnp.float32),
            jax.ShapeDtypeStruct((seq_count, kvh, sub, HEAD_WIDTH), jnp.float32),
        ],
        compiler_params=pltpu.CompilerParams(
            dimension_semantics=("arbitrary", "arbitrary"),
            vmem_limit_bytes=48 * 1024 * 1024,
        ),
    )(live, q4, kv)


def merge_pair(m, l, acc, axis):
    top = jnp.max(m, axis=axis, keepdims=True)
    f = jnp.exp(m - top)
    return (
        jnp.squeeze(top, axis),
        jnp.sum(f * l, axis=axis),
        jnp.sum(f[..., None] * acc, axis=axis),
    )


def body(queries, draft_key_value, kv_cache, cache_lengths, ancestors, dealing, accepted_path):
    local_reqs = kv_cache.shape[0]
    tree_len = queries.shape[1]
    picker = (
        accepted_path[:, :, None] == jnp.arange(tree_len, dtype=jnp.int32)[None, None, :]
    ).astype(jnp.bfloat16)
    kept_entries = jnp.einsum(
        "rit,rtc->ric", picker, draft_key_value, preferred_element_type=jnp.float32
    ).astype(jnp.bfloat16)

    nz, ny, nx, nc = (lax.axis_size(a) for a in ("z", "y", "x", "c"))
    zi, yi, xi, ci = (lax.axis_index(a) for a in ("z", "y", "x", "c"))
    seq_count = nx * nc
    position = xi * nc + ci
    q_cols = queries.shape[2]
    d_cols = draft_key_value.shape[2]

    both = jnp.concatenate([queries, draft_key_value], axis=2)
    held = lax.all_gather(both, "z", axis=0, tiled=True)
    dest_slot = jnp.arange(ny * local_reqs, dtype=jnp.int32) + (zi * ny) * local_reqs
    wanted = dealing[dest_slot]
    src_group = wanted // local_reqs
    pick = (src_group // ny) * local_reqs + wanted % local_reqs
    send = jnp.take(held, pick, axis=0).reshape((ny, local_reqs) + both.shape[1:])
    recv = lax.all_to_all(send, "y", 0, 0, tiled=True)
    my_group = zi * ny + yi
    mine = lax.dynamic_slice_in_dim(dealing, my_group * local_reqs, local_reqs)
    from_y = (mine // local_reqs) % ny
    recv = recv.reshape((ny * local_reqs,) + both.shape[1:])
    own = jnp.take(recv, from_y * local_reqs + jnp.arange(local_reqs, dtype=jnp.int32), axis=0)

    own = lax.all_gather(own, "x", axis=2, tiled=False)
    own = lax.all_gather(own, "c", axis=3, tiled=False)
    own = own.reshape(local_reqs, tree_len, seq_count, q_cols + d_cols)
    full_query = own[..., :q_cols]
    full_draft = own[..., q_cols:]

    positions = kv_cache.shape[1]
    kv_heads = kv_cache.shape[2] // (2 * HEAD_WIDTH)
    groups = q_cols // HEAD_WIDTH
    rows = tree_len * groups

    q4 = (
        full_query.reshape(local_reqs, tree_len, kv_heads, groups, HEAD_WIDTH)
        .transpose(0, 2, 1, 3, 4)
        .reshape(local_reqs, kv_heads, rows, HEAD_WIDTH)
    )
    live = jnp.clip(cache_lengths - position * positions, 0, positions).astype(jnp.int32)
    part_m, part_l, part_acc = local_attention(q4, kv_cache, live, seq_count)
    sub = part_acc.shape[2]
    ml = jnp.stack([part_m[..., 0], part_l[..., 0]], axis=1).reshape(nx, nc, 2, kv_heads * sub)
    acc = part_acc.reshape(nx, nc, kv_heads * sub, HEAD_WIDTH)
    ml = lax.all_to_all(ml, "c", 1, 1, tiled=True)
    acc = lax.all_to_all(acc, "c", 1, 1, tiled=True)
    m1, l1, a1 = merge_pair(ml[:, :, 0], ml[:, :, 1], acc, axis=1)
    ml = jnp.stack([m1, l1], axis=1)
    ml = lax.all_to_all(ml, "x", 0, 0, tiled=True)
    acc = lax.all_to_all(a1, "x", 0, 0, tiled=True)

    per_slot = seq_count // local_reqs
    tok = tree_len // per_slot
    my_slot = position // per_slot
    my_tok0 = (position % per_slot) * tok
    q_slot = lax.dynamic_index_in_dim(full_query, my_slot, 0, keepdims=False)
    q_mine = lax.dynamic_slice_in_dim(q_slot, my_tok0, tok, 0).reshape(
        tok, kv_heads, groups, HEAD_WIDTH
    )
    d_slot = lax.dynamic_index_in_dim(full_draft, my_slot, 0, keepdims=False).reshape(
        tree_len, kv_heads, 2, HEAD_WIDTH
    )
    anc = lax.dynamic_index_in_dim(ancestors, my_slot, 0, keepdims=False)
    anc = lax.dynamic_slice_in_dim(anc, my_tok0, tok, 0)
    allowed = (anc > 0)[None, :, None, :]
    sd = jnp.einsum(
        "tkgd,jkd->ktgj", q_mine, d_slot[:, :, 0], preferred_element_type=jnp.float32
    ) * HEAD_WIDTH ** (-0.5)
    sd = jnp.where(allowed, sd, jnp.float32(NEG))
    md = jnp.max(sd, axis=-1)
    wd = jnp.where(allowed, jnp.exp(sd - md[..., None]), jnp.float32(0.0))
    ld = jnp.sum(wd, axis=-1)
    od = jnp.einsum(
        "ktgj,jkd->ktgd", wd.astype(jnp.bfloat16), d_slot[:, :, 1], preferred_element_type=jnp.float32
    )
    md = md.reshape(1, kv_heads * sub)
    ld = ld.reshape(1, kv_heads * sub)
    od = od.reshape(1, kv_heads * sub, HEAD_WIDTH)

    _, den, num = merge_pair(
        jnp.concatenate([ml[:, 0], md], axis=0),
        jnp.concatenate([ml[:, 1], ld], axis=0),
        jnp.concatenate([acc, od], axis=0),
        axis=0,
    )
    res = num / den[..., None]
    context = (
        res.reshape(kv_heads, tok, groups, HEAD_WIDTH)
        .transpose(1, 0, 2, 3)
        .reshape(tok, kv_heads * groups * HEAD_WIDTH)
        .astype(jnp.bfloat16)
    )
    return (context, kept_entries)


def solution(mesh):
    req, seq = mesh.shape["req"], mesh.shape["seq"]
    nc = 2
    nx = seq // nc
    ny = int(round(req ** 0.5))
    nz = req // ny
    fine = jax.sharding.Mesh(mesh.devices.reshape(nz, ny, nx, nc), ("z", "y", "x", "c"))
    R, S = ("z", "y"), ("x", "c")
    placed = (
        P(R, None, S),
        P(R, None, S),
        P(R, S, None),
        P(R),
        P(R, None, None),
        P(),
        P(R, None),
    )
    return jax.shard_map(
        body,
        mesh=fine,
        in_specs=placed,
        out_specs=(P(R + S, None), P(R, None, S)),
        check_vma=False,
    )
```

```python
import functools

import jax
import jax.numpy as jnp
from jax import lax
from jax.experimental import pallas as pl
from jax.experimental.pallas import tpu as pltpu
from jax.sharding import PartitionSpec as P

HEAD_WIDTH = 128
BLK = 1024
NEG = -1e30


def attn_kernel(live_ref, q_ref, kv_ref, m_ref, l_ref, acc_ref, m_sc, l_sc, acc_sc,
                *, n_blk, scale, groups):
    slot = pl.program_id(0)
    live = live_ref[slot]
    q = jnp.concatenate(
        [q_ref[:, g * HEAD_WIDTH:(g + 1) * HEAD_WIDTH] for g in range(groups)], axis=0
    )
    m_sc[...] = jnp.full(m_sc.shape, NEG, jnp.float32)
    l_sc[...] = jnp.zeros(l_sc.shape, jnp.float32)
    acc_sc[...] = jnp.zeros(acc_sc.shape, jnp.float32)

    def absorb(b, masked):
        keys = kv_ref[b * BLK:(b + 1) * BLK, 0:HEAD_WIDTH]
        vals = kv_ref[b * BLK:(b + 1) * BLK, HEAD_WIDTH:2 * HEAD_WIDTH]
        s = lax.dot_general(
            q, keys, (((1,), (1,)), ((), ())), preferred_element_type=jnp.float32
        ) * scale
        if masked:
            pos = b * BLK + lax.broadcasted_iota(jnp.int32, (1, BLK), 1)
            allowed = pos < live
            s = jnp.where(allowed, s, jnp.float32(NEG))
        mb = jnp.max(s, axis=1, keepdims=True)
        w = jnp.exp(s - mb)
        if masked:
            w = jnp.where(allowed, w, jnp.float32(0.0))
        lb = jnp.sum(w, axis=1, keepdims=True)
        ob = jnp.dot(w.astype(jnp.bfloat16), vals, preferred_element_type=jnp.float32)
        m_old = m_sc[...]
        new_m = jnp.maximum(m_old, mb)
        fa = jnp.exp(m_old - new_m)
        fb = jnp.exp(mb - new_m)
        l_sc[...] = l_sc[...] * fa + lb * fb
        acc_sc[...] = acc_sc[...] * fa + ob * fb
        m_sc[...] = new_m

    for b in range(n_blk):
        lo, hi = b * BLK, (b + 1) * BLK

        @pl.when(live >= hi)
        def _full():
            absorb(b, False)

        @pl.when(jnp.logical_and(live > lo, live < hi))
        def _part():
            absorb(b, True)

    parts = m_ref.shape[0]
    tree_len = q_ref.shape[0]
    tok = tree_len // parts
    for j in range(parts):
        for g in range(groups):
            src = slice(g * tree_len + j * tok, g * tree_len + (j + 1) * tok)
            dst = slice(g * tok, (g + 1) * tok)
            m_ref[j, dst, :] = m_sc[src, :]
            l_ref[j, dst, :] = l_sc[src, :]
            acc_ref[j, dst, :] = acc_sc[src, :]


def local_attention(q_all, kv, live, seq_count):
    slots, kvh, tree_len, _ = q_all.shape
    positions = kv.shape[1]
    groups = (q_all.shape[3] - 2 * HEAD_WIDTH) // HEAD_WIDTH
    rows = tree_len * groups
    per_slot = seq_count // slots
    sub = rows // per_slot
    kern = functools.partial(
        attn_kernel, n_blk=positions // BLK, scale=HEAD_WIDTH ** (-0.5), groups=groups
    )
    grid_spec = pltpu.PrefetchScalarGridSpec(
        num_scalar_prefetch=1,
        grid=(slots, kvh),
        in_specs=[
            pl.BlockSpec((None, None, tree_len, groups * HEAD_WIDTH), lambda i, k, lv: (i, k, 0, 0)),
            pl.BlockSpec((None, positions, 2 * HEAD_WIDTH), lambda i, k, lv: (i, 0, k)),
        ],
        out_specs=[
            pl.BlockSpec((per_slot, None, sub, 1), lambda i, k, lv: (i, k, 0, 0)),
            pl.BlockSpec((per_slot, None, sub, 1), lambda i, k, lv: (i, k, 0, 0)),
            pl.BlockSpec((per_slot, None, sub, HEAD_WIDTH), lambda i, k, lv: (i, k, 0, 0)),
        ],
        scratch_shapes=[
            pltpu.VMEM((rows, 1), jnp.float32),
            pltpu.VMEM((rows, 1), jnp.float32),
            pltpu.VMEM((rows, HEAD_WIDTH), jnp.float32),
        ],
    )
    return pl.pallas_call(
        kern,
        grid_spec=grid_spec,
        out_shape=[
            jax.ShapeDtypeStruct((seq_count, kvh, sub, 1), jnp.float32),
            jax.ShapeDtypeStruct((seq_count, kvh, sub, 1), jnp.float32),
            jax.ShapeDtypeStruct((seq_count, kvh, sub, HEAD_WIDTH), jnp.float32),
        ],
        compiler_params=pltpu.CompilerParams(
            dimension_semantics=("arbitrary", "arbitrary"),
            vmem_limit_bytes=48 * 1024 * 1024,
        ),
    )(live, q_all, kv)


def merge_pair(m, l, acc, axis):
    top = jnp.max(m, axis=axis, keepdims=True)
    f = jnp.exp(m - top)
    return (
        jnp.squeeze(top, axis),
        jnp.sum(f * l, axis=axis),
        jnp.sum(f[..., None] * acc, axis=axis),
    )


def body(queries, draft_key_value, kv_cache, cache_lengths, ancestors, dealing, accepted_path):
    local_reqs = kv_cache.shape[0]
    tree_len = queries.shape[1]
    picker = (
        accepted_path[:, :, None] == jnp.arange(tree_len, dtype=jnp.int32)[None, None, :]
    ).astype(jnp.bfloat16)
    kept_entries = jnp.einsum(
        "rit,rtc->ric", picker, draft_key_value, preferred_element_type=jnp.float32
    ).astype(jnp.bfloat16)

    nz, ny, nx, nc = (lax.axis_size(a) for a in ("z", "y", "x", "c"))
    zi, yi, xi, ci = (lax.axis_index(a) for a in ("z", "y", "x", "c"))
    seq_count = nx * nc
    position = xi * nc + ci
    q_cols = queries.shape[2]
    d_cols = draft_key_value.shape[2]

    both = jnp.concatenate([queries, draft_key_value], axis=2)
    held = lax.all_gather(both, "z", axis=0, tiled=True)
    dest_slot = jnp.arange(ny * local_reqs, dtype=jnp.int32) + (zi * ny) * local_reqs
    wanted = dealing[dest_slot]
    src_group = wanted // local_reqs
    pick = (src_group // ny) * local_reqs + wanted % local_reqs
    send = jnp.take(held, pick, axis=0).reshape((ny, local_reqs) + both.shape[1:])
    recv = lax.all_to_all(send, "y", 0, 0, tiled=True)
    my_group = zi * ny + yi
    mine = lax.dynamic_slice_in_dim(dealing, my_group * local_reqs, local_reqs)
    from_y = (mine // local_reqs) % ny
    recv = recv.reshape((ny * local_reqs,) + both.shape[1:])
    own = jnp.take(recv, from_y * local_reqs + jnp.arange(local_reqs, dtype=jnp.int32), axis=0)

    own = lax.all_gather(own, "x", axis=1, tiled=False)
    own = lax.all_gather(own, "c", axis=2, tiled=False)
    q_all = own.reshape(local_reqs, seq_count, tree_len, q_cols + d_cols)

    positions = kv_cache.shape[1]
    kv_heads = kv_cache.shape[2] // (2 * HEAD_WIDTH)
    groups = q_cols // HEAD_WIDTH
    live = jnp.clip(cache_lengths - position * positions, 0, positions).astype(jnp.int32)
    part_m, part_l, part_acc = local_attention(q_all, kv_cache, live, seq_count)
    sub = part_acc.shape[2]
    ml = jnp.stack([part_m[..., 0], part_l[..., 0]], axis=1).reshape(nx, nc, 2, kv_heads * sub)
    acc = part_acc.reshape(nx, nc, kv_heads * sub, HEAD_WIDTH)
    ml = lax.all_to_all(ml, "c", 1, 1, tiled=True)
    acc = lax.all_to_all(acc, "c", 1, 1, tiled=True)
    m1, l1, a1 = merge_pair(ml[:, :, 0], ml[:, :, 1], acc, axis=1)
    ml = jnp.stack([m1, l1], axis=1)
    x1 = jnp.where(l1[..., None] > 0, a1 / l1[..., None], jnp.float32(0.0)).astype(jnp.bfloat16)
    ml = lax.all_to_all(ml, "x", 0, 0, tiled=True)
    x1 = lax.all_to_all(x1, "x", 0, 0, tiled=True)
    acc = x1.astype(jnp.float32) * ml[:, 1][..., None]

    per_slot = seq_count // local_reqs
    tok = tree_len // per_slot
    my_slot = position // per_slot
    my_tok0 = (position % per_slot) * tok
    mine_all = lax.dynamic_index_in_dim(q_all, my_slot, 0, keepdims=False)
    q_mine = lax.dynamic_slice_in_dim(mine_all[..., :q_cols], my_tok0, tok, 1).reshape(
        kv_heads, tok, groups, HEAD_WIDTH
    )
    d_slot = mine_all[..., q_cols:].reshape(kv_heads, tree_len, 2, HEAD_WIDTH)
    anc = lax.dynamic_index_in_dim(ancestors, my_slot, 0, keepdims=False)
    anc = lax.dynamic_slice_in_dim(anc, my_tok0, tok, 0)
    allowed = (anc > 0)[None, None, :, :]
    sd = jnp.einsum(
        "ktgd,kjd->kgtj", q_mine, d_slot[:, :, 0], preferred_element_type=jnp.float32
    ) * HEAD_WIDTH ** (-0.5)
    sd = jnp.where(allowed, sd, jnp.float32(NEG))
    md = jnp.max(sd, axis=-1)
    wd = jnp.where(allowed, jnp.exp(sd - md[..., None]), jnp.float32(0.0))
    ld = jnp.sum(wd, axis=-1)
    od = jnp.einsum(
        "kgtj,kjd->kgtd", wd.astype(jnp.bfloat16), d_slot[:, :, 1], preferred_element_type=jnp.float32
    )
    md = md.reshape(1, kv_heads * sub)
    ld = ld.reshape(1, kv_heads * sub)
    od = od.reshape(1, kv_heads * sub, HEAD_WIDTH)

    _, den, num = merge_pair(
        jnp.concatenate([ml[:, 0], md], axis=0),
        jnp.concatenate([ml[:, 1], ld], axis=0),
        jnp.concatenate([acc, od], axis=0),
        axis=0,
    )
    res = num / den[..., None]
    context = (
        res.reshape(kv_heads, groups, tok, HEAD_WIDTH)
        .transpose(2, 0, 1, 3)
        .reshape(tok, kv_heads * groups * HEAD_WIDTH)
        .astype(jnp.bfloat16)
    )
    return (context, kept_entries)


def solution(mesh):
    req, seq = mesh.shape["req"], mesh.shape["seq"]
    nc = 2
    nx = seq // nc
    ny = int(round(req ** 0.5))
    nz = req // ny
    fine = jax.sharding.Mesh(mesh.devices.reshape(nz, ny, nx, nc), ("z", "y", "x", "c"))
    R, S = ("z", "y"), ("x", "c")
    placed = (
        P(R, None, S),
        P(R, None, S),
        P(R, S, None),
        P(R),
        P(R, None, None),
        P(),
        P(R, None),
    )
    return jax.shard_map(
        body,
        mesh=fine,
        in_specs=placed,
        out_specs=(P(R + S, None), P(R, None, S)),
        check_vma=False,
    )
```

```python
import functools

import jax
import jax.numpy as jnp
from jax import lax
from jax.experimental import pallas as pl
from jax.experimental.pallas import tpu as pltpu
from jax.sharding import PartitionSpec as P

HEAD_WIDTH = 128
BLK = 1024
NEG = -1e30


def attn_kernel(live_ref, q_ref, kv_ref, m_ref, l_ref, acc_ref, *, n_blk, scale, groups):
    slot = pl.program_id(0)
    live = live_ref[slot]
    tree_len = q_ref.shape[0]
    rows = tree_len * groups
    q = jnp.concatenate([q_ref[:, g * HEAD_WIDTH:(g + 1) * HEAD_WIDTH] for g in range(groups)], axis=0)
    outs_m, outs_l, outs_a = [], [], []
    for c0 in range(0, rows, rows):
        qc = q[c0:c0 + rows]
        run = None
        for b in range(n_blk):
            keys = kv_ref[b * BLK:(b + 1) * BLK, 0:HEAD_WIDTH]
            vals = kv_ref[b * BLK:(b + 1) * BLK, HEAD_WIDTH:2 * HEAD_WIDTH]
            s = lax.dot_general(qc, keys, (((1,), (1,)), ((), ())), preferred_element_type=jnp.float32) * scale
            pos = b * BLK + lax.broadcasted_iota(jnp.int32, (1, BLK), 1)
            bias = jnp.where(pos < live, jnp.float32(0.0), jnp.float32(NEG))
            s = s + bias
            mb = jnp.max(s, axis=1, keepdims=True)
            w = jnp.exp(s - mb)
            lb = jnp.sum(w, axis=1, keepdims=True)
            ob = jnp.dot(w.astype(jnp.bfloat16), vals, preferred_element_type=jnp.float32)
            if run is None:
                run = (mb, lb, ob)
            else:
                rm, rl, ra = run
                nm = jnp.maximum(rm, mb); fa = jnp.exp(rm - nm); fb = jnp.exp(mb - nm)
                run = (nm, rl * fa + lb * fb, ra * fa + ob * fb)
        outs_m.append(run[0]); outs_l.append(run[1]); outs_a.append(run[2])
    rm = jnp.concatenate(outs_m, 0); rl = jnp.concatenate(outs_l, 0); ra = jnp.concatenate(outs_a, 0)
    parts = m_ref.shape[0]
    tok = tree_len // parts
    for j in range(parts):
        for g in range(groups):
            src = slice(g * tree_len + j * tok, g * tree_len + (j + 1) * tok)
            dst = slice(g * tok, (g + 1) * tok)
            m_ref[j, dst, :] = rm[src]
            l_ref[j, dst, :] = rl[src]
            acc_ref[j, dst, :] = ra[src]

def local_attention(q_all, kv, live, seq_count):
    slots, kvh, tree_len, _ = q_all.shape
    positions = kv.shape[1]
    groups = (q_all.shape[3] - 2 * HEAD_WIDTH) // HEAD_WIDTH
    rows = tree_len * groups
    per_slot = seq_count // slots
    sub = rows // per_slot
    kern = functools.partial(attn_kernel, n_blk=positions // BLK, scale=HEAD_WIDTH ** (-0.5), groups=groups)
    grid_spec = pltpu.PrefetchScalarGridSpec(
        num_scalar_prefetch=1, grid=(slots, kvh),
        in_specs=[pl.BlockSpec((None, None, tree_len, groups * HEAD_WIDTH), lambda i, k, lv: (i, k, 0, 0)),
                  pl.BlockSpec((None, positions, 2 * HEAD_WIDTH), lambda i, k, lv: (i, 0, k))],
        out_specs=[pl.BlockSpec((per_slot, None, sub, 1), lambda i, k, lv: (i, k, 0, 0)),
                   pl.BlockSpec((per_slot, None, sub, 1), lambda i, k, lv: (i, k, 0, 0)),
                   pl.BlockSpec((per_slot, None, sub, HEAD_WIDTH), lambda i, k, lv: (i, k, 0, 0))])
    return pl.pallas_call(kern, grid_spec=grid_spec,
        out_shape=[jax.ShapeDtypeStruct((seq_count, kvh, sub, 1), jnp.float32),
                   jax.ShapeDtypeStruct((seq_count, kvh, sub, 1), jnp.float32),
                   jax.ShapeDtypeStruct((seq_count, kvh, sub, HEAD_WIDTH), jnp.float32)],
        compiler_params=pltpu.CompilerParams(dimension_semantics=("arbitrary", "arbitrary"), vmem_limit_bytes=48 * 1024 * 1024),
    )(live, q_all, kv)


def merge_pair(m, l, acc, axis):
    top = jnp.max(m, axis=axis, keepdims=True)
    f = jnp.exp(m - top)
    return (
        jnp.squeeze(top, axis),
        jnp.sum(f * l, axis=axis),
        jnp.sum(f[..., None] * acc, axis=axis),
    )


def body(queries, draft_key_value, kv_cache, cache_lengths, ancestors, dealing, accepted_path):
    local_reqs = kv_cache.shape[0]
    tree_len = queries.shape[1]
    picker = (
        accepted_path[:, :, None] == jnp.arange(tree_len, dtype=jnp.int32)[None, None, :]
    ).astype(jnp.bfloat16)
    kept_entries = jnp.einsum(
        "rit,rtc->ric", picker, draft_key_value, preferred_element_type=jnp.float32
    ).astype(jnp.bfloat16)

    nz, ny, nx, nc = (lax.axis_size(a) for a in ("z", "y", "x", "c"))
    zi, yi, xi, ci = (lax.axis_index(a) for a in ("z", "y", "x", "c"))
    seq_count = nx * nc
    position = xi * nc + ci
    q_cols = queries.shape[2]
    d_cols = draft_key_value.shape[2]

    both = jnp.concatenate([queries, draft_key_value], axis=2)
    held = lax.all_gather(both, "z", axis=0, tiled=True)
    dest_slot = jnp.arange(ny * local_reqs, dtype=jnp.int32) + (zi * ny) * local_reqs
    wanted = dealing[dest_slot]
    src_group = wanted // local_reqs
    pick = (src_group // ny) * local_reqs + wanted % local_reqs
    send = jnp.take(held, pick, axis=0).reshape((ny, local_reqs) + both.shape[1:])
    recv = lax.all_to_all(send, "y", 0, 0, tiled=True)
    my_group = zi * ny + yi
    mine = lax.dynamic_slice_in_dim(dealing, my_group * local_reqs, local_reqs)
    from_y = (mine // local_reqs) % ny
    recv = recv.reshape((ny * local_reqs,) + both.shape[1:])
    own = jnp.take(recv, from_y * local_reqs + jnp.arange(local_reqs, dtype=jnp.int32), axis=0)

    own = lax.all_gather(own, "x", axis=1, tiled=False)
    own = lax.all_gather(own, "c", axis=2, tiled=False)
    q_all = own.reshape(local_reqs, seq_count, tree_len, q_cols + d_cols)

    positions = kv_cache.shape[1]
    kv_heads = kv_cache.shape[2] // (2 * HEAD_WIDTH)
    groups = q_cols // HEAD_WIDTH
    live = jnp.clip(cache_lengths - position * positions, 0, positions).astype(jnp.int32)
    part_m, part_l, part_acc = local_attention(q_all, kv_cache, live, seq_count)
    sub = part_acc.shape[2]
    rows_acc = kv_heads * sub
    stat_rows = rows_acc // HEAD_WIDTH
    pad = (-(rows_acc + 2 * stat_rows)) % 8

    def pack(acc, m, l):
        lead = acc.shape[:-2]
        parts = [acc, m.reshape(lead + (stat_rows, HEAD_WIDTH)), l.reshape(lead + (stat_rows, HEAD_WIDTH))]
        if pad:
            parts.append(jnp.zeros(lead + (pad, HEAD_WIDTH), jnp.float32))
        return jnp.concatenate(parts, axis=-2)

    def unpack(pk):
        lead = pk.shape[:-2]
        acc = pk[..., :rows_acc, :]
        m = pk[..., rows_acc:rows_acc + stat_rows, :].reshape(lead + (rows_acc,))
        l = pk[..., rows_acc + stat_rows:rows_acc + 2 * stat_rows, :].reshape(lead + (rows_acc,))
        return m, l, acc

    pk = pack(
        part_acc.reshape(nx, nc, rows_acc, HEAD_WIDTH),
        part_m.reshape(nx, nc, rows_acc),
        part_l.reshape(nx, nc, rows_acc),
    )
    pk = lax.all_to_all(pk, "c", 1, 1, tiled=True)
    m1, l1, a1 = merge_pair(*unpack(pk), axis=1)
    pk = lax.all_to_all(pack(a1, m1, l1), "x", 0, 0, tiled=True)
    rm, rl, acc = unpack(pk)

    per_slot = seq_count // local_reqs
    tok = tree_len // per_slot
    my_slot = position // per_slot
    my_tok0 = (position % per_slot) * tok
    mine_all = lax.dynamic_index_in_dim(q_all, my_slot, 0, keepdims=False)
    q_mine = lax.dynamic_slice_in_dim(mine_all[..., :q_cols], my_tok0, tok, 1).reshape(
        kv_heads, tok, groups, HEAD_WIDTH
    )
    d_slot = mine_all[..., q_cols:].reshape(kv_heads, tree_len, 2, HEAD_WIDTH)
    anc = lax.dynamic_index_in_dim(ancestors, my_slot, 0, keepdims=False)
    anc = lax.dynamic_slice_in_dim(anc, my_tok0, tok, 0)
    allowed = (anc > 0)[None, None, :, :]
    sd = jnp.einsum(
        "ktgd,kjd->kgtj", q_mine, d_slot[:, :, 0], preferred_element_type=jnp.float32
    ) * HEAD_WIDTH ** (-0.5)
    sd = jnp.where(allowed, sd, jnp.float32(NEG))
    md = jnp.max(sd, axis=-1)
    wd = jnp.where(allowed, jnp.exp(sd - md[..., None]), jnp.float32(0.0))
    ld = jnp.sum(wd, axis=-1)
    od = jnp.einsum(
        "kgtj,kjd->kgtd", wd.astype(jnp.bfloat16), d_slot[:, :, 1], preferred_element_type=jnp.float32
    )
    md = md.reshape(1, kv_heads * sub)
    ld = ld.reshape(1, kv_heads * sub)
    od = od.reshape(1, kv_heads * sub, HEAD_WIDTH)

    _, den, num = merge_pair(
        jnp.concatenate([rm, md], axis=0),
        jnp.concatenate([rl, ld], axis=0),
        jnp.concatenate([acc, od], axis=0),
        axis=0,
    )
    res = num / den[..., None]
    context = (
        res.reshape(kv_heads, groups, tok, HEAD_WIDTH)
        .transpose(2, 0, 1, 3)
        .reshape(tok, kv_heads * groups * HEAD_WIDTH)
        .astype(jnp.bfloat16)
    )
    return (context, kept_entries)


def solution(mesh):
    req, seq = mesh.shape["req"], mesh.shape["seq"]
    nc = 2
    nx = seq // nc
    ny = int(round(req ** 0.5))
    nz = req // ny
    fine = jax.sharding.Mesh(mesh.devices.reshape(nz, ny, nx, nc), ("z", "y", "x", "c"))
    R, S = ("z", "y"), ("x", "c")
    placed = (
        P(R, None, S),
        P(R, None, S),
        P(R, S, None),
        P(R),
        P(R, None, None),
        P(),
        P(R, None),
    )
    return jax.shard_map(
        body,
        mesh=fine,
        in_specs=placed,
        out_specs=(P(R + S, None), P(R, None, S)),
        check_vma=False,
    )
```

```python
import functools

import jax
import jax.numpy as jnp
from jax import lax
from jax.experimental import pallas as pl
from jax.experimental.pallas import tpu as pltpu
from jax.sharding import PartitionSpec as P

HEAD_WIDTH = 128
BLK = 1024
NEG = -1e30


def attn_kernel(live_ref, q_ref, kv_ref, m_ref, l_ref, acc_ref, *, n_blk, scale, groups):
    slot = pl.program_id(0)
    live = live_ref[slot]
    tree_len = q_ref.shape[0]
    rows = tree_len * groups
    q = jnp.concatenate([q_ref[:, g * HEAD_WIDTH:(g + 1) * HEAD_WIDTH] for g in range(groups)], axis=0)
    outs_m, outs_l, outs_a = [], [], []
    for c0 in range(0, rows, rows):
        qc = q[c0:c0 + rows]
        run = None
        for b in range(n_blk):
            keys = kv_ref[b * BLK:(b + 1) * BLK, 0:HEAD_WIDTH]
            vals = kv_ref[b * BLK:(b + 1) * BLK, HEAD_WIDTH:2 * HEAD_WIDTH]
            s = lax.dot_general(qc, keys, (((1,), (1,)), ((), ())), preferred_element_type=jnp.float32) * scale
            pos = b * BLK + lax.broadcasted_iota(jnp.int32, (1, BLK), 1)
            bias = jnp.where(pos < live, jnp.float32(0.0), jnp.float32(NEG))
            s = s + bias
            mb = jnp.max(s, axis=1, keepdims=True)
            w = jnp.exp(s - mb)
            lb = jnp.sum(w, axis=1, keepdims=True)
            ob = jnp.dot(w.astype(jnp.bfloat16), vals, preferred_element_type=jnp.float32)
            if run is None:
                run = (mb, lb, ob)
            else:
                rm, rl, ra = run
                nm = jnp.maximum(rm, mb); fa = jnp.exp(rm - nm); fb = jnp.exp(mb - nm)
                run = (nm, rl * fa + lb * fb, ra * fa + ob * fb)
        outs_m.append(run[0]); outs_l.append(run[1]); outs_a.append(run[2])
    rm = jnp.concatenate(outs_m, 0); rl = jnp.concatenate(outs_l, 0); ra = jnp.concatenate(outs_a, 0)
    parts = m_ref.shape[0]
    tok = tree_len // parts
    for j in range(parts):
        for g in range(groups):
            src = slice(g * tree_len + j * tok, g * tree_len + (j + 1) * tok)
            dst = slice(g * tok, (g + 1) * tok)
            m_ref[j, dst, :] = rm[src]
            l_ref[j, dst, :] = rl[src]
            acc_ref[j, dst, :] = ra[src]

def local_attention(q_all, kv, pref, seq_count, nc):
    slots, kvh, tree_len, _ = q_all.shape
    positions = kv.shape[1]
    groups = (q_all.shape[3] - 2 * HEAD_WIDTH) // HEAD_WIDTH
    rows = tree_len * groups
    per_slot = seq_count // slots
    sub = rows // per_slot
    kern = functools.partial(attn_kernel, n_blk=positions // BLK, scale=HEAD_WIDTH ** (-0.5), groups=groups)
    grid_spec = pltpu.PrefetchScalarGridSpec(
        num_scalar_prefetch=1, grid=(slots, kvh),
        in_specs=[pl.BlockSpec((None, None, tree_len, groups * HEAD_WIDTH), lambda i, k, lv: (i, k, 0, 0)),
                  pl.BlockSpec((None, positions, 2 * HEAD_WIDTH), lambda i, k, lv: (i, 0, k * nc + lv[slots]))],
        out_specs=[pl.BlockSpec((per_slot, None, sub, 1), lambda i, k, lv: (i, k, 0, 0)),
                   pl.BlockSpec((per_slot, None, sub, 1), lambda i, k, lv: (i, k, 0, 0)),
                   pl.BlockSpec((per_slot, None, sub, HEAD_WIDTH), lambda i, k, lv: (i, k, 0, 0))])
    return pl.pallas_call(kern, grid_spec=grid_spec,
        out_shape=[jax.ShapeDtypeStruct((seq_count, kvh, sub, 1), jnp.float32),
                   jax.ShapeDtypeStruct((seq_count, kvh, sub, 1), jnp.float32),
                   jax.ShapeDtypeStruct((seq_count, kvh, sub, HEAD_WIDTH), jnp.float32)],
        compiler_params=pltpu.CompilerParams(dimension_semantics=("arbitrary", "arbitrary"), vmem_limit_bytes=48 * 1024 * 1024),
    )(pref, q_all, kv)


def merge_pair(m, l, acc, axis):
    top = jnp.max(m, axis=axis, keepdims=True)
    f = jnp.exp(m - top)
    return (
        jnp.squeeze(top, axis),
        jnp.sum(f * l, axis=axis),
        jnp.sum(f[..., None] * acc, axis=axis),
    )


def body(queries, draft_key_value, kv_cache, cache_lengths, ancestors, dealing, accepted_path):
    local_reqs = kv_cache.shape[0]
    tree_len = queries.shape[1]
    picker = (
        accepted_path[:, :, None] == jnp.arange(tree_len, dtype=jnp.int32)[None, None, :]
    ).astype(jnp.bfloat16)
    kept_entries = jnp.einsum(
        "rit,rtc->ric", picker, draft_key_value, preferred_element_type=jnp.float32
    ).astype(jnp.bfloat16)

    nz, ny, nx, nc = (lax.axis_size(a) for a in ("z", "y", "x", "c"))
    zi, yi, xi, ci = (lax.axis_index(a) for a in ("z", "y", "x", "c"))
    seq_count = nx * nc
    position = xi * nc + ci
    q_cols = queries.shape[2]
    d_cols = draft_key_value.shape[2]

    both = jnp.concatenate([queries, draft_key_value], axis=2)
    held = lax.all_gather(both, "z", axis=0, tiled=True)
    dest_slot = jnp.arange(ny * local_reqs, dtype=jnp.int32) + (zi * ny) * local_reqs
    wanted = dealing[dest_slot]
    src_group = wanted // local_reqs
    pick = (src_group // ny) * local_reqs + wanted % local_reqs
    send = jnp.take(held, pick, axis=0).reshape((ny, local_reqs) + both.shape[1:])
    recv = lax.all_to_all(send, "y", 0, 0, tiled=True)
    my_group = zi * ny + yi
    mine = lax.dynamic_slice_in_dim(dealing, my_group * local_reqs, local_reqs)
    from_y = (mine // local_reqs) % ny
    recv = recv.reshape((ny * local_reqs,) + both.shape[1:])
    own = jnp.take(recv, from_y * local_reqs + jnp.arange(local_reqs, dtype=jnp.int32), axis=0)

    own_x = lax.all_gather(own, "x", axis=1, tiled=False)
    other_x = lax.ppermute(own_x, "c", perm=[(0, 1), (1, 0)])

    positions = kv_cache.shape[1]
    kv_heads = kv_cache.shape[2] // (2 * HEAD_WIDTH)
    groups = q_cols // HEAD_WIDTH
    live = jnp.clip(cache_lengths - position * positions, 0, positions).astype(jnp.int32)
    pm_a, pl_a, pa_a = local_attention(own_x, kv_cache, jnp.concatenate([live, ci[None]]), seq_count, nc)
    pm_b, pl_b, pa_b = local_attention(
        other_x, kv_cache, jnp.concatenate([live, (1 - ci)[None]]), seq_count, nc
    )
    first = ci == 0

    def by_parity(a, b):
        return jnp.where(first, jnp.concatenate([a, b], axis=1), jnp.concatenate([b, a], axis=1))

    part_m = by_parity(pm_a, pm_b)
    part_l = by_parity(pl_a, pl_b)
    part_acc = by_parity(pa_a, pa_b)
    q_all = jnp.where(
        first, jnp.concatenate([own_x, other_x], axis=1), jnp.concatenate([other_x, own_x], axis=1)
    )
    sub = part_acc.shape[2]
    rows_acc = kv_heads * sub
    stat_rows = rows_acc // HEAD_WIDTH
    pad = (-(rows_acc + 2 * stat_rows)) % 8

    def pack(acc, m, l):
        lead = acc.shape[:-2]
        parts = [acc, m.reshape(lead + (stat_rows, HEAD_WIDTH)), l.reshape(lead + (stat_rows, HEAD_WIDTH))]
        if pad:
            parts.append(jnp.zeros(lead + (pad, HEAD_WIDTH), jnp.float32))
        return jnp.concatenate(parts, axis=-2)

    def unpack(pk):
        lead = pk.shape[:-2]
        acc = pk[..., :rows_acc, :]
        m = pk[..., rows_acc:rows_acc + stat_rows, :].reshape(lead + (rows_acc,))
        l = pk[..., rows_acc + stat_rows:rows_acc + 2 * stat_rows, :].reshape(lead + (rows_acc,))
        return m, l, acc

    pk = pack(
        part_acc.reshape(nx, nc, rows_acc, HEAD_WIDTH),
        part_m.reshape(nx, nc, rows_acc),
        part_l.reshape(nx, nc, rows_acc),
    )
    pk = lax.all_to_all(pk, "c", 1, 1, tiled=True)
    m1, l1, a1 = merge_pair(*unpack(pk), axis=1)
    pk = lax.all_to_all(pack(a1, m1, l1), "x", 0, 0, tiled=True)
    rm, rl, acc = unpack(pk)

    per_slot = seq_count // local_reqs
    tok = tree_len // per_slot
    my_slot = position // per_slot
    my_tok0 = (position % per_slot) * tok
    mine_all = lax.dynamic_index_in_dim(q_all, my_slot, 0, keepdims=False)
    q_mine = lax.dynamic_slice_in_dim(mine_all[..., :q_cols], my_tok0, tok, 1).reshape(
        kv_heads, tok, groups, HEAD_WIDTH
    )
    d_slot = mine_all[..., q_cols:].reshape(kv_heads, tree_len, 2, HEAD_WIDTH)
    anc = lax.dynamic_index_in_dim(ancestors, my_slot, 0, keepdims=False)
    anc = lax.dynamic_slice_in_dim(anc, my_tok0, tok, 0)
    allowed = (anc > 0)[None, None, :, :]
    sd = jnp.einsum(
        "ktgd,kjd->kgtj", q_mine, d_slot[:, :, 0], preferred_element_type=jnp.float32
    ) * HEAD_WIDTH ** (-0.5)
    sd = jnp.where(allowed, sd, jnp.float32(NEG))
    md = jnp.max(sd, axis=-1)
    wd = jnp.where(allowed, jnp.exp(sd - md[..., None]), jnp.float32(0.0))
    ld = jnp.sum(wd, axis=-1)
    od = jnp.einsum(
        "kgtj,kjd->kgtd", wd.astype(jnp.bfloat16), d_slot[:, :, 1], preferred_element_type=jnp.float32
    )
    md = md.reshape(1, kv_heads * sub)
    ld = ld.reshape(1, kv_heads * sub)
    od = od.reshape(1, kv_heads * sub, HEAD_WIDTH)

    _, den, num = merge_pair(
        jnp.concatenate([rm, md], axis=0),
        jnp.concatenate([rl, ld], axis=0),
        jnp.concatenate([acc, od], axis=0),
        axis=0,
    )
    res = num / den[..., None]
    context = (
        res.reshape(nc, kv_heads // nc, groups, tok, HEAD_WIDTH)
        .transpose(3, 1, 0, 2, 4)
        .reshape(tok, kv_heads * groups * HEAD_WIDTH)
        .astype(jnp.bfloat16)
    )
    return (context, kept_entries)


def solution(mesh):
    req, seq = mesh.shape["req"], mesh.shape["seq"]
    nc = 2
    nx = seq // nc
    ny = int(round(req ** 0.5))
    nz = req // ny
    fine = jax.sharding.Mesh(mesh.devices.reshape(nz, ny, nx, nc), ("z", "y", "x", "c"))
    R, S = ("z", "y"), ("x", "c")
    placed = (
        P(R, None, S),
        P(R, None, S),
        P(R, S, None),
        P(R),
        P(R, None, None),
        P(),
        P(R, None),
    )
    return jax.shard_map(
        body,
        mesh=fine,
        in_specs=placed,
        out_specs=(P(R + S, None), P(R, None, S)),
        check_vma=False,
    )
```

```python
import functools

import jax
import jax.numpy as jnp
from jax import lax
from jax.experimental import pallas as pl
from jax.experimental.pallas import tpu as pltpu
from jax.sharding import PartitionSpec as P

HEAD_WIDTH = 128
BLK = 1024
NEG = -1e30


def attn_kernel(live_ref, q_ref, kv_ref, *refs, n_blk, scale, groups):
    m_ref, l_ref, acc_ref = refs[-3:]
    slot = pl.program_id(0)
    live = live_ref[slot]
    tree_len = q_ref.shape[0]
    rows = tree_len * groups
    q = jnp.concatenate(
        [q_ref[:, g * HEAD_WIDTH:(g + 1) * HEAD_WIDTH] for g in range(groups)], axis=0
    )
    run = None
    for b in range(n_blk):
        keys = kv_ref[b * BLK:(b + 1) * BLK, 0:HEAD_WIDTH]
        vals = kv_ref[b * BLK:(b + 1) * BLK, HEAD_WIDTH:2 * HEAD_WIDTH]
        s = lax.dot_general(
            q, keys, (((1,), (1,)), ((), ())), preferred_element_type=jnp.float32
        ) * scale
        pos = b * BLK + lax.broadcasted_iota(jnp.int32, (1, BLK), 1)
        s = s + jnp.where(pos < live, jnp.float32(0.0), jnp.float32(NEG))
        mb = jnp.max(s, axis=1, keepdims=True)
        w = jnp.exp(s - mb)
        lb = jnp.sum(w, axis=1, keepdims=True)
        ob = jnp.dot(w.astype(jnp.bfloat16), vals, preferred_element_type=jnp.float32)
        if run is None:
            run = (mb, lb, ob)
        else:
            rm, rl, ra = run
            nm = jnp.maximum(rm, mb)
            fa = jnp.exp(rm - nm)
            fb = jnp.exp(mb - nm)
            run = (nm, rl * fa + lb * fb, ra * fa + ob * fb)
    rm, rl, ra = run
    m_ref[...] = jnp.transpose(jnp.broadcast_to(rm, (rows, HEAD_WIDTH)))[0:8]
    l_ref[...] = jnp.transpose(jnp.broadcast_to(rl, (rows, HEAD_WIDTH)))[0:8]
    parts = acc_ref.shape[0]
    tok = tree_len // parts
    for j in range(parts):
        for g in range(groups):
            src = slice(g * tree_len + j * tok, g * tree_len + (j + 1) * tok)
            acc_ref[j, g * tok:(g + 1) * tok, :] = ra[src]


def local_attention(q_half, kv, pref, seq_count, nc, prev=None):
    slots, kh, tree_len, cols = q_half.shape
    positions = kv.shape[1]
    groups = (cols - 2 * HEAD_WIDTH) // HEAD_WIDTH
    kvh = kh * nc
    rows = tree_len * groups
    per_slot = seq_count // slots
    sub = rows // per_slot
    kern = functools.partial(
        attn_kernel, n_blk=positions // BLK, scale=HEAD_WIDTH ** (-0.5), groups=groups
    )
    in_specs = [
        pl.BlockSpec((None, None, tree_len, groups * HEAD_WIDTH), lambda i, k, lv: (i, k, 0, 0)),
        pl.BlockSpec((None, positions, 2 * HEAD_WIDTH), lambda i, k, lv: (i, 0, k * nc + lv[slots])),
    ]
    operands = [pref, q_half, kv]
    aliases = {}
    if prev is not None:
        in_specs += [pl.BlockSpec(memory_space=pl.ANY)] * 3
        operands += list(prev)
        aliases = {3: 0, 4: 1, 5: 2}
    grid_spec = pltpu.PrefetchScalarGridSpec(
        num_scalar_prefetch=1,
        grid=(slots, kh),
        in_specs=in_specs,
        out_specs=[
            pl.BlockSpec((None, None, 8, rows), lambda i, k, lv: (i, lv[slots] * kh + k, 0, 0)),
            pl.BlockSpec((None, None, 8, rows), lambda i, k, lv: (i, lv[slots] * kh + k, 0, 0)),
            pl.BlockSpec(
                (per_slot, None, sub, HEAD_WIDTH), lambda i, k, lv: (i, lv[slots] * kh + k, 0, 0)
            ),
        ],
    )
    return pl.pallas_call(
        kern,
        grid_spec=grid_spec,
        out_shape=[
            jax.ShapeDtypeStruct((slots, kvh, 8, rows), jnp.float32),
            jax.ShapeDtypeStruct((slots, kvh, 8, rows), jnp.float32),
            jax.ShapeDtypeStruct((seq_count, kvh, sub, HEAD_WIDTH), jnp.float32),
        ],
        input_output_aliases=aliases,
        compiler_params=pltpu.CompilerParams(
            dimension_semantics=("arbitrary", "arbitrary"),
            vmem_limit_bytes=48 * 1024 * 1024,
        ),
    )(*operands)


def merge_pair(m, l, acc, axis):
    top = jnp.max(m, axis=axis, keepdims=True)
    f = jnp.exp(m - top)
    return (
        jnp.squeeze(top, axis),
        jnp.sum(f * l, axis=axis),
        jnp.sum(f[..., None] * acc, axis=axis),
    )


def body(queries, draft_key_value, kv_cache, cache_lengths, ancestors, dealing, accepted_path):
    local_reqs = kv_cache.shape[0]
    tree_len = queries.shape[1]
    picker = (
        accepted_path[:, :, None] == jnp.arange(tree_len, dtype=jnp.int32)[None, None, :]
    ).astype(jnp.bfloat16)
    kept_entries = jnp.einsum(
        "rit,rtc->ric", picker, draft_key_value, preferred_element_type=jnp.float32
    ).astype(jnp.bfloat16)

    nz, ny, nx, nc = (lax.axis_size(a) for a in ("z", "y", "x", "c"))
    zi, yi, xi, ci = (lax.axis_index(a) for a in ("z", "y", "x", "c"))
    seq_count = nx * nc
    position = xi * nc + ci
    q_cols = queries.shape[2]
    d_cols = draft_key_value.shape[2]

    both = jnp.concatenate([queries, draft_key_value], axis=2)
    held = lax.all_gather(both, "z", axis=0, tiled=True)
    dest_slot = jnp.arange(ny * local_reqs, dtype=jnp.int32) + (zi * ny) * local_reqs
    wanted = dealing[dest_slot]
    src_group = wanted // local_reqs
    pick = (src_group // ny) * local_reqs + wanted % local_reqs
    send = jnp.take(held, pick, axis=0).reshape((ny, local_reqs) + both.shape[1:])
    recv = lax.all_to_all(send, "y", 0, 0, tiled=True)
    my_group = zi * ny + yi
    mine = lax.dynamic_slice_in_dim(dealing, my_group * local_reqs, local_reqs)
    from_y = (mine // local_reqs) % ny
    recv = recv.reshape((ny * local_reqs,) + both.shape[1:])
    own = jnp.take(recv, from_y * local_reqs + jnp.arange(local_reqs, dtype=jnp.int32), axis=0)

    own_x = lax.all_gather(own, "x", axis=1, tiled=False)
    other_x = lax.ppermute(own_x, "c", perm=[(0, 1), (1, 0)])

    positions = kv_cache.shape[1]
    kv_heads = kv_cache.shape[2] // (2 * HEAD_WIDTH)
    groups = q_cols // HEAD_WIDTH
    live = jnp.clip(cache_lengths - position * positions, 0, positions).astype(jnp.int32)
    first_out = local_attention(own_x, kv_cache, jnp.concatenate([live, ci[None]]), seq_count, nc)
    m_rows, l_rows, part_acc = local_attention(
        other_x, kv_cache, jnp.concatenate([live, (1 - ci)[None]]), seq_count, nc, prev=first_out
    )
    first = ci == 0
    per_slot = seq_count // local_reqs
    tok = tree_len // per_slot

    def dest_major(rows_arr):
        r = rows_arr[:, :, 0, :].reshape(local_reqs, kv_heads, groups, per_slot, tok)
        return r.transpose(0, 3, 1, 2, 4).reshape(seq_count, kv_heads, groups * tok)

    part_m = dest_major(m_rows)
    part_l = dest_major(l_rows)
    sub = part_acc.shape[2]
    rows_acc = kv_heads * sub
    stat_rows = rows_acc // HEAD_WIDTH
    pad = (-(rows_acc + 2 * stat_rows)) % 8

    def pack(acc, m, l):
        lead = acc.shape[:-2]
        parts = [acc, m.reshape(lead + (stat_rows, HEAD_WIDTH)), l.reshape(lead + (stat_rows, HEAD_WIDTH))]
        if pad:
            parts.append(jnp.zeros(lead + (pad, HEAD_WIDTH), jnp.float32))
        return jnp.concatenate(parts, axis=-2)

    def unpack(pk):
        lead = pk.shape[:-2]
        acc = pk[..., :rows_acc, :]
        m = pk[..., rows_acc:rows_acc + stat_rows, :].reshape(lead + (rows_acc,))
        l = pk[..., rows_acc + stat_rows:rows_acc + 2 * stat_rows, :].reshape(lead + (rows_acc,))
        return m, l, acc

    pk = pack(
        part_acc.reshape(nx, nc, rows_acc, HEAD_WIDTH),
        part_m.reshape(nx, nc, rows_acc),
        part_l.reshape(nx, nc, rows_acc),
    )
    pk = lax.all_to_all(pk, "c", 1, 1, tiled=True)
    m1, l1, a1 = merge_pair(*unpack(pk), axis=1)
    pk = lax.all_to_all(pack(a1, m1, l1), "x", 0, 0, tiled=True)
    rm, rl, acc = unpack(pk)

    my_slot = position // per_slot
    my_tok0 = (position % per_slot) * tok
    mine_own = lax.dynamic_index_in_dim(own_x, my_slot, 0, keepdims=False)
    mine_other = lax.dynamic_index_in_dim(other_x, my_slot, 0, keepdims=False)
    mine_all = jnp.where(
        first,
        jnp.concatenate([mine_own, mine_other], axis=0),
        jnp.concatenate([mine_other, mine_own], axis=0),
    )
    q_mine = lax.dynamic_slice_in_dim(mine_all[..., :q_cols], my_tok0, tok, 1).reshape(
        kv_heads, tok, groups, HEAD_WIDTH
    )
    d_slot = mine_all[..., q_cols:].reshape(kv_heads, tree_len, 2, HEAD_WIDTH)
    anc = lax.dynamic_index_in_dim(ancestors, my_slot, 0, keepdims=False)
    anc = lax.dynamic_slice_in_dim(anc, my_tok0, tok, 0)
    allowed = (anc > 0)[None, None, :, :]
    sd = jnp.einsum(
        "ktgd,kjd->kgtj", q_mine, d_slot[:, :, 0], preferred_element_type=jnp.float32
    ) * HEAD_WIDTH ** (-0.5)
    sd = jnp.where(allowed, sd, jnp.float32(NEG))
    md = jnp.max(sd, axis=-1)
    wd = jnp.where(allowed, jnp.exp(sd - md[..., None]), jnp.float32(0.0))
    ld = jnp.sum(wd, axis=-1)
    od = jnp.einsum(
        "kgtj,kjd->kgtd", wd.astype(jnp.bfloat16), d_slot[:, :, 1], preferred_element_type=jnp.float32
    )
    md = md.reshape(1, kv_heads * sub)
    ld = ld.reshape(1, kv_heads * sub)
    od = od.reshape(1, kv_heads * sub, HEAD_WIDTH)

    _, den, num = merge_pair(
        jnp.concatenate([rm, md], axis=0),
        jnp.concatenate([rl, ld], axis=0),
        jnp.concatenate([acc, od], axis=0),
        axis=0,
    )
    res = num / den[..., None]
    context = (
        res.reshape(nc, kv_heads // nc, groups, tok, HEAD_WIDTH)
        .transpose(3, 1, 0, 2, 4)
        .reshape(tok, kv_heads * groups * HEAD_WIDTH)
        .astype(jnp.bfloat16)
    )
    return (context, kept_entries)


def solution(mesh):
    req, seq = mesh.shape["req"], mesh.shape["seq"]
    nc = 2
    nx = seq // nc
    ny = int(round(req ** 0.5))
    nz = req // ny
    fine = jax.sharding.Mesh(mesh.devices.reshape(nz, ny, nx, nc), ("z", "y", "x", "c"))
    R, S = ("z", "y"), ("x", "c")
    placed = (
        P(R, None, S),
        P(R, None, S),
        P(R, S, None),
        P(R),
        P(R, None, None),
        P(),
        P(R, None),
    )
    return jax.shard_map(
        body,
        mesh=fine,
        in_specs=placed,
        out_specs=(P(R + S, None), P(R, None, S)),
        check_vma=False,
    )
```

```python
import functools

import jax
import jax.numpy as jnp
from jax import lax
from jax.experimental import pallas as pl
from jax.experimental.pallas import tpu as pltpu
from jax.sharding import PartitionSpec as P

HEAD_WIDTH = 128
BLK = 1024
NEG = -1e30


def attn_kernel(live_ref, q_ref, kv_ref, *refs, n_blk, scale, groups):
    m_ref, l_ref, acc_ref = refs[-3:]
    slot = pl.program_id(0)
    live = live_ref[slot]
    tree_len = q_ref.shape[0]
    rows = tree_len * groups
    q = jnp.concatenate(
        [q_ref[:, g * HEAD_WIDTH:(g + 1) * HEAD_WIDTH] for g in range(groups)], axis=0
    )
    def blocks(masked):
        run = None
        for b in range(n_blk):
            keys = kv_ref[b * BLK:(b + 1) * BLK, 0:HEAD_WIDTH]
            vals = kv_ref[b * BLK:(b + 1) * BLK, HEAD_WIDTH:2 * HEAD_WIDTH]
            s = lax.dot_general(
                q, keys, (((1,), (1,)), ((), ())), preferred_element_type=jnp.float32
            ) * scale
            if masked:
                pos = b * BLK + lax.broadcasted_iota(jnp.int32, (1, BLK), 1)
                s = s + jnp.where(pos < live, jnp.float32(0.0), jnp.float32(NEG))
            mb = jnp.max(s, axis=1, keepdims=True)
            w = jnp.exp(s - mb)
            lb = jnp.sum(w, axis=1, keepdims=True)
            ob = jnp.dot(w.astype(jnp.bfloat16), vals, preferred_element_type=jnp.float32)
            if run is None:
                run = (mb, lb, ob)
            else:
                rm, rl, ra = run
                nm = jnp.maximum(rm, mb)
                fa = jnp.exp(rm - nm)
                fb = jnp.exp(mb - nm)
                run = (nm, rl * fa + lb * fb, ra * fa + ob * fb)
        write(*run)

    def write(rm, rl, ra):
        m_ref[...] = jnp.transpose(jnp.broadcast_to(rm, (rows, HEAD_WIDTH)))[0:8]
        l_ref[...] = jnp.transpose(jnp.broadcast_to(rl, (rows, HEAD_WIDTH)))[0:8]
        parts = acc_ref.shape[0]
        tok = tree_len // parts
        for j in range(parts):
            for g in range(groups):
                src = slice(g * tree_len + j * tok, g * tree_len + (j + 1) * tok)
                acc_ref[j, g * tok:(g + 1) * tok, :] = ra[src]

    full = live >= n_blk * BLK

    @pl.when(full)
    def _full():
        blocks(False)

    @pl.when(jnp.logical_not(full))
    def _part():
        blocks(True)


def local_attention(q_half, kv, pref, seq_count, nc, prev=None):
    slots, kh, tree_len, cols = q_half.shape
    positions = kv.shape[1]
    groups = (cols - 2 * HEAD_WIDTH) // HEAD_WIDTH
    kvh = kh * nc
    rows = tree_len * groups
    per_slot = seq_count // slots
    sub = rows // per_slot
    kern = functools.partial(
        attn_kernel, n_blk=positions // BLK, scale=HEAD_WIDTH ** (-0.5), groups=groups
    )
    in_specs = [
        pl.BlockSpec((None, None, tree_len, groups * HEAD_WIDTH), lambda i, k, lv: (i, k, 0, 0)),
        pl.BlockSpec((None, positions, 2 * HEAD_WIDTH), lambda i, k, lv: (i, 0, k * nc + lv[slots])),
    ]
    operands = [pref, q_half, kv]
    aliases = {}
    if prev is not None:
        in_specs += [pl.BlockSpec(memory_space=pl.ANY)] * 3
        operands += list(prev)
        aliases = {3: 0, 4: 1, 5: 2}
    grid_spec = pltpu.PrefetchScalarGridSpec(
        num_scalar_prefetch=1,
        grid=(slots, kh),
        in_specs=in_specs,
        out_specs=[
            pl.BlockSpec((None, None, 8, rows), lambda i, k, lv: (i, lv[slots] * kh + k, 0, 0)),
            pl.BlockSpec((None, None, 8, rows), lambda i, k, lv: (i, lv[slots] * kh + k, 0, 0)),
            pl.BlockSpec(
                (per_slot, None, sub, HEAD_WIDTH), lambda i, k, lv: (i, lv[slots] * kh + k, 0, 0)
            ),
        ],
    )
    return pl.pallas_call(
        kern,
        grid_spec=grid_spec,
        out_shape=[
            jax.ShapeDtypeStruct((slots, kvh, 8, rows), jnp.float32),
            jax.ShapeDtypeStruct((slots, kvh, 8, rows), jnp.float32),
            jax.ShapeDtypeStruct((seq_count, kvh, sub, HEAD_WIDTH), jnp.float32),
        ],
        input_output_aliases=aliases,
        compiler_params=pltpu.CompilerParams(
            dimension_semantics=("arbitrary", "arbitrary"),
            vmem_limit_bytes=48 * 1024 * 1024,
        ),
    )(*operands)


def merge_pair(m, l, acc, axis):
    top = jnp.max(m, axis=axis, keepdims=True)
    f = jnp.exp(m - top)
    return (
        jnp.squeeze(top, axis),
        jnp.sum(f * l, axis=axis),
        jnp.sum(f[..., None] * acc, axis=axis),
    )


def body(queries, draft_key_value, kv_cache, cache_lengths, ancestors, dealing, accepted_path):
    local_reqs = kv_cache.shape[0]
    tree_len = queries.shape[1]
    picker = (
        accepted_path[:, :, None] == jnp.arange(tree_len, dtype=jnp.int32)[None, None, :]
    ).astype(jnp.bfloat16)
    kept_entries = jnp.einsum(
        "rit,rtc->ric", picker, draft_key_value, preferred_element_type=jnp.float32
    ).astype(jnp.bfloat16)

    nz, ny, nx, nc = (lax.axis_size(a) for a in ("z", "y", "x", "c"))
    zi, yi, xi, ci = (lax.axis_index(a) for a in ("z", "y", "x", "c"))
    seq_count = nx * nc
    position = xi * nc + ci
    q_cols = queries.shape[2]
    d_cols = draft_key_value.shape[2]

    both = jnp.concatenate([queries, draft_key_value], axis=2)
    held = lax.all_gather(both, "z", axis=0, tiled=True)
    dest_slot = jnp.arange(ny * local_reqs, dtype=jnp.int32) + (zi * ny) * local_reqs
    wanted = dealing[dest_slot]
    src_group = wanted // local_reqs
    pick = (src_group // ny) * local_reqs + wanted % local_reqs
    send = jnp.take(held, pick, axis=0).reshape((ny, local_reqs) + both.shape[1:])
    recv = lax.all_to_all(send, "y", 0, 0, tiled=True)
    my_group = zi * ny + yi
    mine = lax.dynamic_slice_in_dim(dealing, my_group * local_reqs, local_reqs)
    from_y = (mine // local_reqs) % ny
    recv = recv.reshape((ny * local_reqs,) + both.shape[1:])
    own = jnp.take(recv, from_y * local_reqs + jnp.arange(local_reqs, dtype=jnp.int32), axis=0)

    own_x = lax.all_gather(own, "x", axis=1, tiled=False)
    other_x = lax.ppermute(own_x, "c", perm=[(0, 1), (1, 0)])

    positions = kv_cache.shape[1]
    kv_heads = kv_cache.shape[2] // (2 * HEAD_WIDTH)
    groups = q_cols // HEAD_WIDTH
    live = jnp.clip(cache_lengths - position * positions, 0, positions).astype(jnp.int32)
    first_out = local_attention(own_x, kv_cache, jnp.concatenate([live, ci[None]]), seq_count, nc)
    m_rows, l_rows, part_acc = local_attention(
        other_x, kv_cache, jnp.concatenate([live, (1 - ci)[None]]), seq_count, nc, prev=first_out
    )
    first = ci == 0
    per_slot = seq_count // local_reqs
    tok = tree_len // per_slot

    def dest_major(rows_arr):
        r = rows_arr[:, :, 0, :].reshape(local_reqs, kv_heads, groups, per_slot, tok)
        return r.transpose(0, 3, 1, 2, 4).reshape(seq_count, kv_heads, groups * tok)

    part_m = dest_major(m_rows)
    part_l = dest_major(l_rows)
    sub = part_acc.shape[2]
    rows_acc = kv_heads * sub
    stat_rows = rows_acc // HEAD_WIDTH
    pad = (-(rows_acc + 2 * stat_rows)) % 8

    def pack(acc, m, l):
        lead = acc.shape[:-2]
        parts = [acc, m.reshape(lead + (stat_rows, HEAD_WIDTH)), l.reshape(lead + (stat_rows, HEAD_WIDTH))]
        if pad:
            parts.append(jnp.zeros(lead + (pad, HEAD_WIDTH), jnp.float32))
        return jnp.concatenate(parts, axis=-2)

    def unpack(pk):
        lead = pk.shape[:-2]
        acc = pk[..., :rows_acc, :]
        m = pk[..., rows_acc:rows_acc + stat_rows, :].reshape(lead + (rows_acc,))
        l = pk[..., rows_acc + stat_rows:rows_acc + 2 * stat_rows, :].reshape(lead + (rows_acc,))
        return m, l, acc

    pk = pack(
        part_acc.reshape(nx, nc, rows_acc, HEAD_WIDTH),
        part_m.reshape(nx, nc, rows_acc),
        part_l.reshape(nx, nc, rows_acc),
    )
    pk = lax.all_to_all(pk, "c", 1, 1, tiled=True)
    m1, l1, a1 = merge_pair(*unpack(pk), axis=1)
    pk = lax.all_to_all(pack(a1, m1, l1), "x", 0, 0, tiled=True)
    rm, rl, acc = unpack(pk)

    my_slot = position // per_slot
    my_tok0 = (position % per_slot) * tok
    mine_own = lax.dynamic_index_in_dim(own_x, my_slot, 0, keepdims=False)
    mine_other = lax.dynamic_index_in_dim(other_x, my_slot, 0, keepdims=False)
    mine_all = jnp.where(
        first,
        jnp.concatenate([mine_own, mine_other], axis=0),
        jnp.concatenate([mine_other, mine_own], axis=0),
    )
    q_mine = lax.dynamic_slice_in_dim(mine_all[..., :q_cols], my_tok0, tok, 1).reshape(
        kv_heads, tok, groups, HEAD_WIDTH
    )
    d_slot = mine_all[..., q_cols:].reshape(kv_heads, tree_len, 2, HEAD_WIDTH)
    anc = lax.dynamic_index_in_dim(ancestors, my_slot, 0, keepdims=False)
    anc = lax.dynamic_slice_in_dim(anc, my_tok0, tok, 0)
    allowed = (anc > 0)[None, None, :, :]
    sd = jnp.einsum(
        "ktgd,kjd->kgtj", q_mine, d_slot[:, :, 0], preferred_element_type=jnp.float32
    ) * HEAD_WIDTH ** (-0.5)
    sd = jnp.where(allowed, sd, jnp.float32(NEG))
    md = jnp.max(sd, axis=-1)
    wd = jnp.where(allowed, jnp.exp(sd - md[..., None]), jnp.float32(0.0))
    ld = jnp.sum(wd, axis=-1)
    od = jnp.einsum(
        "kgtj,kjd->kgtd", wd.astype(jnp.bfloat16), d_slot[:, :, 1], preferred_element_type=jnp.float32
    )
    md = md.reshape(1, kv_heads * sub)
    ld = ld.reshape(1, kv_heads * sub)
    od = od.reshape(1, kv_heads * sub, HEAD_WIDTH)

    _, den, num = merge_pair(
        jnp.concatenate([rm, md], axis=0),
        jnp.concatenate([rl, ld], axis=0),
        jnp.concatenate([acc, od], axis=0),
        axis=0,
    )
    res = num / den[..., None]
    context = (
        res.reshape(nc, kv_heads // nc, groups, tok, HEAD_WIDTH)
        .transpose(3, 1, 0, 2, 4)
        .reshape(tok, kv_heads * groups * HEAD_WIDTH)
        .astype(jnp.bfloat16)
    )
    return (context, kept_entries)


def solution(mesh):
    req, seq = mesh.shape["req"], mesh.shape["seq"]
    nc = 2
    nx = seq // nc
    ny = int(round(req ** 0.5))
    nz = req // ny
    fine = jax.sharding.Mesh(mesh.devices.reshape(nz, ny, nx, nc), ("z", "y", "x", "c"))
    R, S = ("z", "y"), ("x", "c")
    placed = (
        P(R, None, S),
        P(R, None, S),
        P(R, S, None),
        P(R),
        P(R, None, None),
        P(),
        P(R, None),
    )
    return jax.shard_map(
        body,
        mesh=fine,
        in_specs=placed,
        out_specs=(P(R + S, None), P(R, None, S)),
        check_vma=False,
    )
```

```python
import functools

import jax
import jax.numpy as jnp
from jax import lax
from jax.experimental import pallas as pl
from jax.experimental.pallas import tpu as pltpu
from jax.sharding import PartitionSpec as P


HEAD_WIDTH = 128
BLK = 1024
NEG = -1e30


def attn_kernel(live_ref, q_ref, kv_ref, *refs, n_blk, scale, groups):
    m_ref, l_ref, acc_ref = refs[-3:]
    slot = pl.program_id(0)
    live = live_ref[slot]
    tree_len = q_ref.shape[0]
    rows = tree_len * groups
    q = jnp.concatenate(
        [q_ref[:, g * HEAD_WIDTH:(g + 1) * HEAD_WIDTH] for g in range(groups)], axis=0
    )
    run = None
    for b in range(n_blk):
        keys = kv_ref[b * BLK:(b + 1) * BLK, 0:HEAD_WIDTH]
        vals = kv_ref[b * BLK:(b + 1) * BLK, HEAD_WIDTH:2 * HEAD_WIDTH]
        s = lax.dot_general(
            q, keys, (((1,), (1,)), ((), ())), preferred_element_type=jnp.float32
        ) * scale
        pos = b * BLK + lax.broadcasted_iota(jnp.int32, (1, BLK), 1)
        s = s + jnp.where(pos < live, jnp.float32(0.0), jnp.float32(NEG))
        mb = jnp.max(s, axis=1, keepdims=True)
        w = jnp.exp(s - mb)
        lb = jnp.sum(w, axis=1, keepdims=True)
        ob = jnp.dot(w.astype(jnp.bfloat16), vals, preferred_element_type=jnp.float32)
        if run is None:
            run = (mb, lb, ob)
        else:
            rm, rl, ra = run
            nm = jnp.maximum(rm, mb)
            fa = jnp.exp(rm - nm)
            fb = jnp.exp(mb - nm)
            run = (nm, rl * fa + lb * fb, ra * fa + ob * fb)
    rm, rl, ra = run
    m_ref[...] = jnp.transpose(jnp.broadcast_to(rm, (rows, HEAD_WIDTH)))[0:8]
    l_ref[...] = jnp.transpose(jnp.broadcast_to(rl, (rows, HEAD_WIDTH)))[0:8]
    parts = acc_ref.shape[0]
    tok = tree_len // parts
    for j in range(parts):
        for g in range(groups):
            src = slice(g * tree_len + j * tok, g * tree_len + (j + 1) * tok)
            acc_ref[j, g * tok:(g + 1) * tok, :] = ra[src]


def local_attention(q_half, kv, pref, seq_count, nc, prev=None):
    slots, kh, tree_len, cols = q_half.shape
    positions = kv.shape[1]
    groups = (cols - 2 * HEAD_WIDTH) // HEAD_WIDTH
    rows = tree_len * groups
    per_slot = seq_count // slots
    sub = rows // per_slot
    kern = functools.partial(
        attn_kernel, n_blk=positions // BLK, scale=HEAD_WIDTH ** (-0.5), groups=groups
    )
    in_specs = [
        pl.BlockSpec((None, None, tree_len, groups * HEAD_WIDTH), lambda i, k, lv: (i, k, 0, 0)),
        pl.BlockSpec((None, positions, 2 * HEAD_WIDTH), lambda i, k, lv: (i, 0, k * nc + lv[slots])),
    ]
    operands = [pref, q_half, kv]
    aliases = {}
    if prev is not None:
        in_specs += [pl.BlockSpec(memory_space=pl.ANY)] * 3
        operands += list(prev)
        aliases = {3: 0, 4: 1, 5: 2}
    grid_spec = pltpu.PrefetchScalarGridSpec(
        num_scalar_prefetch=1,
        grid=(slots, kh),
        in_specs=in_specs,
        out_specs=[
            pl.BlockSpec((None, None, 8, rows), lambda i, k, lv: (i, k, 0, 0)),
            pl.BlockSpec((None, None, 8, rows), lambda i, k, lv: (i, k, 0, 0)),
            pl.BlockSpec(
                (per_slot, None, sub, HEAD_WIDTH), lambda i, k, lv: (i, k, 0, 0)
            ),
        ],
    )
    return pl.pallas_call(
        kern,
        grid_spec=grid_spec,
        out_shape=[
            jax.ShapeDtypeStruct((slots, kh, 8, rows), jnp.float32),
            jax.ShapeDtypeStruct((slots, kh, 8, rows), jnp.float32),
            jax.ShapeDtypeStruct((seq_count, kh, sub, HEAD_WIDTH), jnp.float32),
        ],
        input_output_aliases=aliases,
        compiler_params=pltpu.CompilerParams(
            dimension_semantics=("arbitrary", "arbitrary"),
            vmem_limit_bytes=48 * 1024 * 1024,
        ),
    )(*operands)


def merge_pair(m, l, acc, axis):
    top = jnp.max(m, axis=axis, keepdims=True)
    f = jnp.exp(m - top)
    return (
        jnp.squeeze(top, axis),
        jnp.sum(f * l, axis=axis),
        jnp.sum(f[..., None] * acc, axis=axis),
    )


def body_inner(queries, draft_key_value, kv_cache, cache_lengths, ancestors, dealing, accepted_path):
    local_reqs = kv_cache.shape[0]
    tree_len = queries.shape[1]
    picker = (
        accepted_path[:, :, None] == jnp.arange(tree_len, dtype=jnp.int32)[None, None, :]
    ).astype(jnp.bfloat16)
    kept_entries = jnp.einsum(
        "rit,rtc->ric", picker, draft_key_value, preferred_element_type=jnp.float32
    ).astype(jnp.bfloat16)

    _, ny, nx, nc = (lax.axis_size(a) for a in ("z", "y", "x", "c"))
    zi, yi, xi, ci = (lax.axis_index(a) for a in ("z", "y", "x", "c"))
    seq_count = nx * nc
    position = xi * nc + ci
    q_cols = queries.shape[2]

    both = jnp.concatenate([queries, draft_key_value], axis=2)
    held = lax.all_gather(both, "z", axis=0, tiled=True)
    dest_slot = jnp.arange(ny * local_reqs, dtype=jnp.int32) + (zi * ny) * local_reqs
    wanted = dealing[dest_slot]
    src_group = wanted // local_reqs
    pick = (src_group // ny) * local_reqs + wanted % local_reqs
    send = jnp.take(held, pick, axis=0).reshape((ny, local_reqs) + both.shape[1:])
    recv = lax.all_to_all(send, "y", 0, 0, tiled=True)
    my_group = zi * ny + yi
    mine = lax.dynamic_slice_in_dim(dealing, my_group * local_reqs, local_reqs)
    from_y = (mine // local_reqs) % ny
    recv = recv.reshape((ny * local_reqs,) + both.shape[1:])
    own = jnp.take(recv, from_y * local_reqs + jnp.arange(local_reqs, dtype=jnp.int32), axis=0)

    own_x = lax.all_gather(own, "x", axis=1, tiled=False)
    other_x = lax.ppermute(own_x, "c", perm=[(0, 1), (1, 0)])

    positions = kv_cache.shape[1]
    kv_heads = kv_cache.shape[2] // (2 * HEAD_WIDTH)
    groups = q_cols // HEAD_WIDTH
    live = jnp.clip(cache_lengths - position * positions, 0, positions).astype(jnp.int32)
    per_slot = seq_count // local_reqs
    tok = tree_len // per_slot
    kh = kv_heads // nc
    rows_acc = kh * groups * tok
    stat_rows = rows_acc // HEAD_WIDTH
    pad = (-(rows_acc + 2 * stat_rows)) % 8

    def dest_major(rows_arr):
        r = rows_arr[:, :, 0, :].reshape(local_reqs, kh, groups, per_slot, tok)
        return r.transpose(0, 3, 1, 2, 4).reshape(seq_count, rows_acc)

    def pack(acc, m, l):
        lead = acc.shape[:-2]
        parts = [acc, m.reshape(lead + (stat_rows, HEAD_WIDTH)), l.reshape(lead + (stat_rows, HEAD_WIDTH))]
        if pad:
            parts.append(jnp.zeros(lead + (pad, HEAD_WIDTH), jnp.float32))
        return jnp.concatenate(parts, axis=-2)

    def unpack(pk):
        lead = pk.shape[:-2]
        acc = pk[..., :rows_acc, :]
        m = pk[..., rows_acc:rows_acc + stat_rows, :].reshape(lead + (rows_acc,))
        l = pk[..., rows_acc + stat_rows:rows_acc + 2 * stat_rows, :].reshape(lead + (rows_acc,))
        return m, l, acc

    def packed(out):
        m_rows, l_rows, acc = out
        pk = pack(acc.reshape(seq_count, rows_acc, HEAD_WIDTH), dest_major(m_rows), dest_major(l_rows))
        return pk.reshape((nx, nc) + pk.shape[1:])

    def split_c(pk):
        mine = lax.dynamic_index_in_dim(pk, ci, 1, keepdims=False)
        theirs = lax.dynamic_index_in_dim(pk, 1 - ci, 1, keepdims=False)
        return mine, theirs

    swap = [(0, 1), (1, 0)]
    pk_a = packed(local_attention(own_x, kv_cache, jnp.concatenate([live, ci[None]]), seq_count, nc))
    mine_a, theirs_a = split_c(pk_a)
    theirs_a, mine_a, other_b = lax.optimization_barrier((theirs_a, mine_a, other_x))
    got_a = lax.ppermute(theirs_a, "c", perm=swap)
    pref_b = jnp.concatenate([live, (1 - ci)[None]])
    out_b = local_attention(other_b, kv_cache, pref_b, seq_count, nc)
    pk_b = packed(out_b)
    mine_b, theirs_b = split_c(pk_b)
    got_b = lax.ppermute(theirs_b, "c", perm=swap)

    m_c, l_c, a_c = merge_pair(*(jnp.stack(t, 1) for t in zip(unpack(mine_a), unpack(got_b))), axis=1)
    m_o, l_o, a_o = merge_pair(*(jnp.stack(t, 1) for t in zip(unpack(mine_b), unpack(got_a))), axis=1)
    merged = jnp.concatenate([pack(a_c, m_c, l_c), pack(a_o, m_o, l_o)], axis=1)
    pk = lax.all_to_all(merged, "x", 0, 0, tiled=True)
    half = pk.shape[1] // 2
    rm_c, rl_c, acc_c = unpack(pk[:, :half])
    rm_o, rl_o, acc_o = unpack(pk[:, half:])
    rm = jnp.concatenate([rm_c, rm_o], axis=1)
    rl = jnp.concatenate([rl_c, rl_o], axis=1)
    acc = jnp.concatenate([acc_c, acc_o], axis=1)
    sub = groups * tok

    my_slot = position // per_slot
    my_tok0 = (position % per_slot) * tok
    mine_own = lax.dynamic_index_in_dim(own_x, my_slot, 0, keepdims=False)
    mine_other = lax.dynamic_index_in_dim(other_x, my_slot, 0, keepdims=False)
    mine_all = jnp.concatenate([mine_own, mine_other], axis=0)
    q_mine = lax.dynamic_slice_in_dim(mine_all[..., :q_cols], my_tok0, tok, 1).reshape(
        kv_heads, tok, groups, HEAD_WIDTH
    )
    d_slot = mine_all[..., q_cols:].reshape(kv_heads, tree_len, 2, HEAD_WIDTH)
    anc = lax.dynamic_index_in_dim(ancestors, my_slot, 0, keepdims=False)
    anc = lax.dynamic_slice_in_dim(anc, my_tok0, tok, 0)
    allowed = (anc > 0)[None, None, :, :]
    sd = jnp.einsum(
        "ktgd,kjd->kgtj", q_mine, d_slot[:, :, 0], preferred_element_type=jnp.float32
    ) * HEAD_WIDTH ** (-0.5)
    sd = jnp.where(allowed, sd, jnp.float32(NEG))
    md = jnp.max(sd, axis=-1)
    wd = jnp.where(allowed, jnp.exp(sd - md[..., None]), jnp.float32(0.0))
    ld = jnp.sum(wd, axis=-1)
    od = jnp.einsum(
        "kgtj,kjd->kgtd", wd.astype(jnp.bfloat16), d_slot[:, :, 1], preferred_element_type=jnp.float32
    )
    md = md.reshape(1, kv_heads * sub)
    ld = ld.reshape(1, kv_heads * sub)
    od = od.reshape(1, kv_heads * sub, HEAD_WIDTH)

    _, den, num = merge_pair(
        jnp.concatenate([rm, md], axis=0),
        jnp.concatenate([rl, ld], axis=0),
        jnp.concatenate([acc, od], axis=0),
        axis=0,
    )
    res = (num / den[..., None]).reshape(nc, kh, groups, tok, HEAD_WIDTH)
    res = jnp.where(ci == 0, res, res[::-1])
    context = (
        res.transpose(3, 1, 0, 2, 4)
        .reshape(tok, kv_heads * groups * HEAD_WIDTH)
        .astype(jnp.bfloat16)
    )
    return (context, kept_entries)


def solution(mesh):
    req, seq = mesh.shape["req"], mesh.shape["seq"]
    nc = 2
    nx = seq // nc
    ny = int(round(req ** 0.5))
    nz = req // ny
    fine = jax.sharding.Mesh(mesh.devices.reshape(nz, ny, nx, nc), ("z", "y", "x", "c"))
    R, S = ("z", "y"), ("x", "c")
    placed = (
        P(R, None, S),
        P(R, None, S),
        P(R, S, None),
        P(R),
        P(R, None, None),
        P(),
        P(R, None),
    )
    return jax.shard_map(
        body_inner,
        mesh=fine,
        in_specs=placed,
        out_specs=(P(R + S, None), P(R, None, S)),
        check_vma=False,
    )
```

```python
import functools

import jax
import jax.numpy as jnp
from jax import lax
from jax.experimental import pallas as pl
from jax.experimental.pallas import tpu as pltpu
from jax.sharding import PartitionSpec as P

HEAD_WIDTH = 128
BLK = 1024
NEG = -1e30


def attn_kernel(live_ref, q_ref, kv_ref, *refs, n_blk, scale, groups):
    m_ref, l_ref, acc_ref = refs[-3:]
    slot = pl.program_id(0)
    live = live_ref[slot]
    tree_len = q_ref.shape[0]
    rows = tree_len * groups
    q = jnp.concatenate(
        [q_ref[:, g * HEAD_WIDTH:(g + 1) * HEAD_WIDTH] for g in range(groups)], axis=0
    )
    run = None
    for b in range(n_blk):
        keys = kv_ref[b * BLK:(b + 1) * BLK, 0:HEAD_WIDTH]
        vals = kv_ref[b * BLK:(b + 1) * BLK, HEAD_WIDTH:2 * HEAD_WIDTH]
        s = lax.dot_general(
            q, keys, (((1,), (1,)), ((), ())), preferred_element_type=jnp.float32
        ) * scale
        pos = b * BLK + lax.broadcasted_iota(jnp.int32, (1, BLK), 1)
        s = s + jnp.where(pos < live, jnp.float32(0.0), jnp.float32(NEG))
        mb = jnp.max(s, axis=1, keepdims=True)
        w = jnp.exp(s - mb)
        lb = jnp.sum(w, axis=1, keepdims=True)
        ob = jnp.dot(w.astype(jnp.bfloat16), vals, preferred_element_type=jnp.float32)
        if run is None:
            run = (mb, lb, ob)
        else:
            rm, rl, ra = run
            nm = jnp.maximum(rm, mb)
            fa = jnp.exp(rm - nm)
            fb = jnp.exp(mb - nm)
            run = (nm, rl * fa + lb * fb, ra * fa + ob * fb)
    rm, rl, ra = run
    m_ref[...] = jnp.transpose(jnp.broadcast_to(rm, (rows, HEAD_WIDTH)))[0:8]
    l_ref[...] = jnp.transpose(jnp.broadcast_to(rl, (rows, HEAD_WIDTH)))[0:8]
    parts = acc_ref.shape[0]
    tok = tree_len // parts
    for j in range(parts):
        for g in range(groups):
            src = slice(g * tree_len + j * tok, g * tree_len + (j + 1) * tok)
            acc_ref[j, g * tok:(g + 1) * tok, :] = ra[src]


def local_attention(q_half, kv, pref, seq_count, nc, prev=None):
    slots, kh, tree_len, cols = q_half.shape
    positions = kv.shape[1]
    groups = (cols - 2 * HEAD_WIDTH) // HEAD_WIDTH
    kvh = kh * nc
    rows = tree_len * groups
    per_slot = seq_count // slots
    sub = rows // per_slot
    kern = functools.partial(
        attn_kernel, n_blk=positions // BLK, scale=HEAD_WIDTH ** (-0.5), groups=groups
    )
    in_specs = [
        pl.BlockSpec((None, None, tree_len, groups * HEAD_WIDTH), lambda i, k, lv: (i, k, 0, 0)),
        pl.BlockSpec((None, positions, 2 * HEAD_WIDTH), lambda i, k, lv: (i, 0, k * nc + lv[slots])),
    ]
    operands = [pref, q_half, kv]
    aliases = {}
    if prev is not None:
        in_specs += [pl.BlockSpec(memory_space=pl.ANY)] * 3
        operands += list(prev)
        aliases = {3: 0, 4: 1, 5: 2}
    grid_spec = pltpu.PrefetchScalarGridSpec(
        num_scalar_prefetch=1,
        grid=(slots, kh),
        in_specs=in_specs,
        out_specs=[
            pl.BlockSpec((None, None, 8, rows), lambda i, k, lv: (i, lv[slots] * kh + k, 0, 0)),
            pl.BlockSpec((None, None, 8, rows), lambda i, k, lv: (i, lv[slots] * kh + k, 0, 0)),
            pl.BlockSpec(
                (per_slot, None, sub, HEAD_WIDTH), lambda i, k, lv: (i, lv[slots] * kh + k, 0, 0)
            ),
        ],
    )
    return pl.pallas_call(
        kern,
        grid_spec=grid_spec,
        out_shape=[
            jax.ShapeDtypeStruct((slots, kvh, 8, rows), jnp.float32),
            jax.ShapeDtypeStruct((slots, kvh, 8, rows), jnp.float32),
            jax.ShapeDtypeStruct((seq_count, kvh, sub, HEAD_WIDTH), jnp.float32),
        ],
        input_output_aliases=aliases,
        compiler_params=pltpu.CompilerParams(
            dimension_semantics=("arbitrary", "arbitrary"),
            vmem_limit_bytes=48 * 1024 * 1024,
        ),
    )(*operands)


def merge_pair(m, l, acc, axis):
    top = jnp.max(m, axis=axis, keepdims=True)
    f = jnp.exp(m - top)
    return (
        jnp.squeeze(top, axis),
        jnp.sum(f * l, axis=axis),
        jnp.sum(f[..., None] * acc, axis=axis),
    )


def body(queries, draft_key_value, kv_cache, cache_lengths, ancestors, dealing, accepted_path):
    local_reqs = kv_cache.shape[0]
    tree_len = queries.shape[1]
    picker = (
        accepted_path[:, :, None] == jnp.arange(tree_len, dtype=jnp.int32)[None, None, :]
    ).astype(jnp.bfloat16)
    kept_entries = jnp.einsum(
        "rit,rtc->ric", picker, draft_key_value, preferred_element_type=jnp.float32
    ).astype(jnp.bfloat16)

    nz, ny, nx, nc = (lax.axis_size(a) for a in ("z", "y", "x", "c"))
    zi, yi, xi, ci = (lax.axis_index(a) for a in ("z", "y", "x", "c"))
    seq_count = nx * nc
    position = xi * nc + ci
    q_cols = queries.shape[2]
    d_cols = draft_key_value.shape[2]

    both = jnp.concatenate([queries, draft_key_value], axis=2)
    held = lax.all_gather(both, "z", axis=0, tiled=True)
    dest_slot = jnp.arange(ny * local_reqs, dtype=jnp.int32) + (zi * ny) * local_reqs
    wanted = dealing[dest_slot]
    src_group = wanted // local_reqs
    pick = (src_group // ny) * local_reqs + wanted % local_reqs
    send = jnp.take(held, pick, axis=0).reshape((ny, local_reqs) + both.shape[1:])
    recv = lax.all_to_all(send, "y", 0, 0, tiled=True)
    my_group = zi * ny + yi
    mine = lax.dynamic_slice_in_dim(dealing, my_group * local_reqs, local_reqs)
    from_y = (mine // local_reqs) % ny
    recv = recv.reshape((ny * local_reqs,) + both.shape[1:])
    own = jnp.take(recv, from_y * local_reqs + jnp.arange(local_reqs, dtype=jnp.int32), axis=0)

    own_x = lax.all_gather(own, "x", axis=1, tiled=False)
    other_x = lax.ppermute(own_x, "c", perm=[(0, 1), (1, 0)])

    positions = kv_cache.shape[1]
    kv_heads = kv_cache.shape[2] // (2 * HEAD_WIDTH)
    groups = q_cols // HEAD_WIDTH
    live = jnp.clip(cache_lengths - position * positions, 0, positions).astype(jnp.int32)
    first_out = local_attention(own_x, kv_cache, jnp.concatenate([live, ci[None]]), seq_count, nc)
    m_rows, l_rows, part_acc = local_attention(
        other_x, kv_cache, jnp.concatenate([live, (1 - ci)[None]]), seq_count, nc, prev=first_out
    )
    first = ci == 0
    per_slot = seq_count // local_reqs
    tok = tree_len // per_slot

    def dest_major(rows_arr):
        r = rows_arr[:, :, 0, :].reshape(local_reqs, kv_heads, groups, per_slot, tok)
        return r.transpose(0, 3, 1, 2, 4).reshape(seq_count, kv_heads, groups * tok)

    part_m = dest_major(m_rows)
    part_l = dest_major(l_rows)
    sub = part_acc.shape[2]
    rows_acc = kv_heads * sub
    stat_rows = rows_acc // HEAD_WIDTH
    pad = (-(rows_acc + 2 * stat_rows)) % 8

    def pack(acc, m, l):
        lead = acc.shape[:-2]
        parts = [acc, m.reshape(lead + (stat_rows, HEAD_WIDTH)), l.reshape(lead + (stat_rows, HEAD_WIDTH))]
        if pad:
            parts.append(jnp.zeros(lead + (pad, HEAD_WIDTH), jnp.float32))
        return jnp.concatenate(parts, axis=-2)

    def unpack(pk):
        lead = pk.shape[:-2]
        acc = pk[..., :rows_acc, :]
        m = pk[..., rows_acc:rows_acc + stat_rows, :].reshape(lead + (rows_acc,))
        l = pk[..., rows_acc + stat_rows:rows_acc + 2 * stat_rows, :].reshape(lead + (rows_acc,))
        return m, l, acc

    pk = pack(
        part_acc.reshape(nx, nc, rows_acc, HEAD_WIDTH),
        part_m.reshape(nx, nc, rows_acc),
        part_l.reshape(nx, nc, rows_acc),
    )
    pk = lax.all_to_all(pk, "c", 1, 1, tiled=True)
    m1, l1, a1 = merge_pair(*unpack(pk), axis=1)
    send = pack(a1, m1, l1)
    pieces = [lax.dynamic_index_in_dim(send, xi, 0, keepdims=False)]
    for shift in range(1, nx):
        piece = lax.dynamic_index_in_dim(send, (xi + shift) % nx, 0, keepdims=False)
        pieces.append(lax.ppermute(piece, "x", perm=[(i, (i + shift) % nx) for i in range(nx)]))
    pk = jnp.stack(pieces, axis=0)
    rm, rl, acc = unpack(pk)

    my_slot = position // per_slot
    my_tok0 = (position % per_slot) * tok
    mine_own = lax.dynamic_index_in_dim(own_x, my_slot, 0, keepdims=False)
    mine_other = lax.dynamic_index_in_dim(other_x, my_slot, 0, keepdims=False)
    mine_all = jnp.where(
        first,
        jnp.concatenate([mine_own, mine_other], axis=0),
        jnp.concatenate([mine_other, mine_own], axis=0),
    )
    q_mine = lax.dynamic_slice_in_dim(mine_all[..., :q_cols], my_tok0, tok, 1).reshape(
        kv_heads, tok, groups, HEAD_WIDTH
    )
    d_slot = mine_all[..., q_cols:].reshape(kv_heads, tree_len, 2, HEAD_WIDTH)
    anc = lax.dynamic_index_in_dim(ancestors, my_slot, 0, keepdims=False)
    anc = lax.dynamic_slice_in_dim(anc, my_tok0, tok, 0)
    allowed = (anc > 0)[None, None, :, :]
    sd = jnp.einsum(
        "ktgd,kjd->kgtj", q_mine, d_slot[:, :, 0], preferred_element_type=jnp.float32
    ) * HEAD_WIDTH ** (-0.5)
    sd = jnp.where(allowed, sd, jnp.float32(NEG))
    md = jnp.max(sd, axis=-1)
    wd = jnp.where(allowed, jnp.exp(sd - md[..., None]), jnp.float32(0.0))
    ld = jnp.sum(wd, axis=-1)
    od = jnp.einsum(
        "kgtj,kjd->kgtd", wd.astype(jnp.bfloat16), d_slot[:, :, 1], preferred_element_type=jnp.float32
    )
    md = md.reshape(1, kv_heads * sub)
    ld = ld.reshape(1, kv_heads * sub)
    od = od.reshape(1, kv_heads * sub, HEAD_WIDTH)

    _, den, num = merge_pair(
        jnp.concatenate([rm, md], axis=0),
        jnp.concatenate([rl, ld], axis=0),
        jnp.concatenate([acc, od], axis=0),
        axis=0,
    )
    res = num / den[..., None]
    context = (
        res.reshape(nc, kv_heads // nc, groups, tok, HEAD_WIDTH)
        .transpose(3, 1, 0, 2, 4)
        .reshape(tok, kv_heads * groups * HEAD_WIDTH)
        .astype(jnp.bfloat16)
    )
    return (context, kept_entries)


def solution(mesh):
    req, seq = mesh.shape["req"], mesh.shape["seq"]
    nc = 2
    nx = seq // nc
    ny = int(round(req ** 0.5))
    nz = req // ny
    fine = jax.sharding.Mesh(mesh.devices.reshape(nz, ny, nx, nc), ("z", "y", "x", "c"))
    R, S = ("z", "y"), ("x", "c")
    placed = (
        P(R, None, S),
        P(R, None, S),
        P(R, S, None),
        P(R),
        P(R, None, None),
        P(),
        P(R, None),
    )
    return jax.shard_map(
        body,
        mesh=fine,
        in_specs=placed,
        out_specs=(P(R + S, None), P(R, None, S)),
        check_vma=False,
    )
```

```python
import functools

import jax
import jax.numpy as jnp
from jax import lax
from jax.experimental import pallas as pl
from jax.experimental.pallas import tpu as pltpu
from jax.sharding import PartitionSpec as P

HEAD_WIDTH = 128
BLK = 1024
NEG = -1e30


def attn_kernel(live_ref, q_ref, kv_ref, *refs, n_blk, scale, groups):
    m_ref, l_ref, acc_ref = refs[-3:]
    slot = pl.program_id(0)
    live = live_ref[slot]
    tree_len = q_ref.shape[0]
    rows = tree_len * groups
    q = jnp.concatenate(
        [q_ref[:, g * HEAD_WIDTH:(g + 1) * HEAD_WIDTH] for g in range(groups)], axis=0
    )
    run = None
    for b in range(n_blk):
        keys = kv_ref[b * BLK:(b + 1) * BLK, 0:HEAD_WIDTH]
        vals = kv_ref[b * BLK:(b + 1) * BLK, HEAD_WIDTH:2 * HEAD_WIDTH]
        s = lax.dot_general(
            q, keys, (((1,), (1,)), ((), ())), preferred_element_type=jnp.float32
        ) * scale
        pos = b * BLK + lax.broadcasted_iota(jnp.int32, (1, BLK), 1)
        s = s + jnp.where(pos < live, jnp.float32(0.0), jnp.float32(NEG))
        mb = jnp.max(s, axis=1, keepdims=True)
        w = jnp.exp(s - mb)
        lb = jnp.sum(w, axis=1, keepdims=True)
        ob = jnp.dot(w.astype(jnp.bfloat16), vals, preferred_element_type=jnp.float32)
        if run is None:
            run = (mb, lb, ob)
        else:
            rm, rl, ra = run
            nm = jnp.maximum(rm, mb)
            fa = jnp.exp(rm - nm)
            fb = jnp.exp(mb - nm)
            run = (nm, rl * fa + lb * fb, ra * fa + ob * fb)
    rm, rl, ra = run
    parts = acc_ref.shape[0]
    tok = tree_len // parts
    gap = jnp.zeros((HEAD_WIDTH - groups * tok, 1), jnp.float32)

    def lane_rows(col, out_ref):
        pieces = []
        for j in range(parts):
            for g in range(groups):
                pieces.append(col[g * tree_len + j * tok:g * tree_len + (j + 1) * tok])
            pieces.append(gap)
        wide = jnp.concatenate(pieces, axis=0)
        flat = jnp.transpose(jnp.broadcast_to(wide, (parts * HEAD_WIDTH, HEAD_WIDTH)))[0:1]
        for j in range(parts):
            out_ref[j:j + 1, :] = flat[:, j * HEAD_WIDTH:(j + 1) * HEAD_WIDTH]

    lane_rows(rm, m_ref)
    lane_rows(rl, l_ref)
    for j in range(parts):
        for g in range(groups):
            src = slice(g * tree_len + j * tok, g * tree_len + (j + 1) * tok)
            acc_ref[j, g * tok:(g + 1) * tok, :] = ra[src]


def local_attention(q_half, kv, pref, seq_count, nc, prev=None):
    slots, kh, tree_len, cols = q_half.shape
    positions = kv.shape[1]
    groups = (cols - 2 * HEAD_WIDTH) // HEAD_WIDTH
    kvh = kh * nc
    rows = tree_len * groups
    per_slot = seq_count // slots
    sub = rows // per_slot
    kern = functools.partial(
        attn_kernel, n_blk=positions // BLK, scale=HEAD_WIDTH ** (-0.5), groups=groups
    )
    in_specs = [
        pl.BlockSpec((None, None, tree_len, groups * HEAD_WIDTH), lambda i, k, lv: (i, k, 0, 0)),
        pl.BlockSpec((None, positions, 2 * HEAD_WIDTH), lambda i, k, lv: (i, 0, k * nc + lv[slots])),
    ]
    operands = [pref, q_half, kv]
    aliases = {}
    if prev is not None:
        in_specs += [pl.BlockSpec(memory_space=pl.ANY)] * 3
        operands += list(prev)
        aliases = {3: 0, 4: 1, 5: 2}
    grid_spec = pltpu.PrefetchScalarGridSpec(
        num_scalar_prefetch=1,
        grid=(slots, kh),
        in_specs=in_specs,
        out_specs=[
            pl.BlockSpec((None, None, per_slot, HEAD_WIDTH), lambda i, k, lv: (lv[slots] * kh + k, i, 0, 0)),
            pl.BlockSpec((None, None, per_slot, HEAD_WIDTH), lambda i, k, lv: (lv[slots] * kh + k, i, 0, 0)),
            pl.BlockSpec(
                (per_slot, None, sub, HEAD_WIDTH), lambda i, k, lv: (i, lv[slots] * kh + k, 0, 0)
            ),
        ],
    )
    return pl.pallas_call(
        kern,
        grid_spec=grid_spec,
        out_shape=[
            jax.ShapeDtypeStruct((kvh, slots, per_slot, HEAD_WIDTH), jnp.float32),
            jax.ShapeDtypeStruct((kvh, slots, per_slot, HEAD_WIDTH), jnp.float32),
            jax.ShapeDtypeStruct((seq_count, kvh, sub, HEAD_WIDTH), jnp.float32),
        ],
        input_output_aliases=aliases,
        compiler_params=pltpu.CompilerParams(
            dimension_semantics=("arbitrary", "arbitrary"),
            vmem_limit_bytes=48 * 1024 * 1024,
        ),
    )(*operands)


def merge_pair(m, l, acc, axis):
    top = jnp.max(m, axis=axis, keepdims=True)
    f = jnp.exp(m - top)
    return (
        jnp.squeeze(top, axis),
        jnp.sum(f * l, axis=axis),
        jnp.sum(f[..., None] * acc, axis=axis),
    )


def body(queries, draft_key_value, kv_cache, cache_lengths, ancestors, dealing, accepted_path):
    local_reqs = kv_cache.shape[0]
    tree_len = queries.shape[1]
    picker = (
        accepted_path[:, :, None] == jnp.arange(tree_len, dtype=jnp.int32)[None, None, :]
    ).astype(jnp.bfloat16)
    kept_entries = jnp.einsum(
        "rit,rtc->ric", picker, draft_key_value, preferred_element_type=jnp.float32
    ).astype(jnp.bfloat16)

    nz, ny, nx, nc = (lax.axis_size(a) for a in ("z", "y", "x", "c"))
    zi, yi, xi, ci = (lax.axis_index(a) for a in ("z", "y", "x", "c"))
    seq_count = nx * nc
    position = xi * nc + ci
    q_cols = queries.shape[2]
    d_cols = draft_key_value.shape[2]

    both = jnp.concatenate([queries, draft_key_value], axis=2)
    held = lax.all_gather(both, "z", axis=0, tiled=True)
    dest_slot = jnp.arange(ny * local_reqs, dtype=jnp.int32) + (zi * ny) * local_reqs
    wanted = dealing[dest_slot]
    src_group = wanted // local_reqs
    pick = (src_group // ny) * local_reqs + wanted % local_reqs
    send = jnp.take(held, pick, axis=0).reshape((ny, local_reqs) + both.shape[1:])
    recv = lax.all_to_all(send, "y", 0, 0, tiled=True)
    my_group = zi * ny + yi
    mine = lax.dynamic_slice_in_dim(dealing, my_group * local_reqs, local_reqs)
    from_y = (mine // local_reqs) % ny
    recv = recv.reshape((ny * local_reqs,) + both.shape[1:])
    own = jnp.take(recv, from_y * local_reqs + jnp.arange(local_reqs, dtype=jnp.int32), axis=0)

    own_x = lax.all_gather(own, "x", axis=1, tiled=False)
    other_x = lax.ppermute(own_x, "c", perm=[(0, 1), (1, 0)])

    positions = kv_cache.shape[1]
    kv_heads = kv_cache.shape[2] // (2 * HEAD_WIDTH)
    groups = q_cols // HEAD_WIDTH
    live = jnp.clip(cache_lengths - position * positions, 0, positions).astype(jnp.int32)
    first_out = local_attention(own_x, kv_cache, jnp.concatenate([live, ci[None]]), seq_count, nc)
    m_rows, l_rows, part_acc = local_attention(
        other_x, kv_cache, jnp.concatenate([live, (1 - ci)[None]]), seq_count, nc, prev=first_out
    )
    first = ci == 0
    per_slot = seq_count // local_reqs
    tok = tree_len // per_slot
    sub = part_acc.shape[2]
    rows_acc = kv_heads * sub

    def dest_rows(r):
        return r.reshape(kv_heads, seq_count, HEAD_WIDTH).transpose(1, 0, 2).reshape(
            nx, nc, kv_heads, HEAD_WIDTH
        )

    def pack(acc, m, l):
        return jnp.concatenate([acc, m, l], axis=-2)

    def unpack(pk):
        acc = pk[..., :rows_acc, :]
        m = pk[..., rows_acc:rows_acc + kv_heads, :sub]
        l = pk[..., rows_acc + kv_heads:, :sub]
        lead = pk.shape[:-2]
        return m.reshape(lead + (rows_acc,)), l.reshape(lead + (rows_acc,)), acc

    def rows_of(v):
        lead = v.shape[:-1]
        v = v.reshape(lead + (kv_heads, sub))
        return jnp.pad(v, [(0, 0)] * len(lead) + [(0, 0), (0, HEAD_WIDTH - sub)])

    pk = pack(part_acc.reshape(nx, nc, rows_acc, HEAD_WIDTH), dest_rows(m_rows), dest_rows(l_rows))
    pk = lax.all_to_all(pk, "c", 1, 1, tiled=True)
    m1, l1, a1 = merge_pair(*unpack(pk), axis=1)
    pk = lax.all_to_all(pack(a1, rows_of(m1), rows_of(l1)), "x", 0, 0, tiled=True)
    rm, rl, acc = unpack(pk)

    my_slot = position // per_slot
    my_tok0 = (position % per_slot) * tok
    mine_own = lax.dynamic_index_in_dim(own_x, my_slot, 0, keepdims=False)
    mine_other = lax.dynamic_index_in_dim(other_x, my_slot, 0, keepdims=False)
    mine_all = jnp.where(
        first,
        jnp.concatenate([mine_own, mine_other], axis=0),
        jnp.concatenate([mine_other, mine_own], axis=0),
    )
    q_mine = lax.dynamic_slice_in_dim(mine_all[..., :q_cols], my_tok0, tok, 1).reshape(
        kv_heads, tok, groups, HEAD_WIDTH
    )
    d_slot = mine_all[..., q_cols:].reshape(kv_heads, tree_len, 2, HEAD_WIDTH)
    anc = lax.dynamic_index_in_dim(ancestors, my_slot, 0, keepdims=False)
    anc = lax.dynamic_slice_in_dim(anc, my_tok0, tok, 0)
    allowed = (anc > 0)[None, None, :, :]
    sd = jnp.einsum(
        "ktgd,kjd->kgtj", q_mine, d_slot[:, :, 0], preferred_element_type=jnp.float32
    ) * HEAD_WIDTH ** (-0.5)
    sd = jnp.where(allowed, sd, jnp.float32(NEG))
    md = jnp.max(sd, axis=-1)
    wd = jnp.where(allowed, jnp.exp(sd - md[..., None]), jnp.float32(0.0))
    ld = jnp.sum(wd, axis=-1)
    od = jnp.einsum(
        "kgtj,kjd->kgtd", wd.astype(jnp.bfloat16), d_slot[:, :, 1], preferred_element_type=jnp.float32
    )
    md = md.reshape(1, kv_heads * sub)
    ld = ld.reshape(1, kv_heads * sub)
    od = od.reshape(1, kv_heads * sub, HEAD_WIDTH)

    _, den, num = merge_pair(
        jnp.concatenate([rm, md], axis=0),
        jnp.concatenate([rl, ld], axis=0),
        jnp.concatenate([acc, od], axis=0),
        axis=0,
    )
    res = num / den[..., None]
    context = (
        res.reshape(nc, kv_heads // nc, groups, tok, HEAD_WIDTH)
        .transpose(3, 1, 0, 2, 4)
        .reshape(tok, kv_heads * groups * HEAD_WIDTH)
        .astype(jnp.bfloat16)
    )
    return (context, kept_entries)


def solution(mesh):
    req, seq = mesh.shape["req"], mesh.shape["seq"]
    nc = 2
    nx = seq // nc
    ny = int(round(req ** 0.5))
    nz = req // ny
    fine = jax.sharding.Mesh(mesh.devices.reshape(nz, ny, nx, nc), ("z", "y", "x", "c"))
    R, S = ("z", "y"), ("x", "c")
    placed = (
        P(R, None, S),
        P(R, None, S),
        P(R, S, None),
        P(R),
        P(R, None, None),
        P(),
        P(R, None),
    )
    return jax.shard_map(
        body,
        mesh=fine,
        in_specs=placed,
        out_specs=(P(R + S, None), P(R, None, S)),
        check_vma=False,
    )
```

```python
import functools

import jax
import jax.numpy as jnp
from jax import lax
from jax.experimental import pallas as pl
from jax.experimental.pallas import tpu as pltpu
from jax.sharding import PartitionSpec as P

HEAD_WIDTH = 128
BLK = 1024
NEG = -1e30


def attn_kernel(live_ref, q_ref, kv_ref, *refs, n_blk, scale, groups):
    m_ref, l_ref, acc_ref = refs[-3:]
    slot = pl.program_id(0)
    live = live_ref[slot]
    tree_len = q_ref.shape[0]
    rows = tree_len * groups
    q = jnp.concatenate(
        [q_ref[:, g * HEAD_WIDTH:(g + 1) * HEAD_WIDTH] for g in range(groups)], axis=0
    )
    run = None
    for b in range(n_blk):
        keys = kv_ref[b * BLK:(b + 1) * BLK, 0:HEAD_WIDTH]
        vals = kv_ref[b * BLK:(b + 1) * BLK, HEAD_WIDTH:2 * HEAD_WIDTH]
        s = lax.dot_general(
            q, keys, (((1,), (1,)), ((), ())), preferred_element_type=jnp.float32
        ) * scale
        pos = b * BLK + lax.broadcasted_iota(jnp.int32, (1, BLK), 1)
        allowed = pos < live
        s = jnp.where(allowed, s, jnp.float32(NEG))
        mb = jnp.max(s, axis=1, keepdims=True)
        w = jnp.where(allowed, jnp.exp(s - mb), jnp.float32(0.0))
        lb = jnp.sum(w, axis=1, keepdims=True)
        ob = jnp.dot(w.astype(jnp.bfloat16), vals, preferred_element_type=jnp.float32)
        if run is None:
            run = (mb, lb, ob)
        else:
            rm, rl, ra = run
            nm = jnp.maximum(rm, mb)
            fa = jnp.exp(rm - nm)
            fb = jnp.exp(mb - nm)
            run = (nm, rl * fa + lb * fb, ra * fa + ob * fb)
    rm, rl, ra = run
    m_ref[...] = jnp.transpose(jnp.broadcast_to(rm, (rows, HEAD_WIDTH)))[0:8]
    l_ref[...] = jnp.transpose(jnp.broadcast_to(rl, (rows, HEAD_WIDTH)))[0:8]
    parts = acc_ref.shape[0]
    tok = tree_len // parts
    for j in range(parts):
        for g in range(groups):
            src = slice(g * tree_len + j * tok, g * tree_len + (j + 1) * tok)
            acc_ref[j, g * tok:(g + 1) * tok, :] = ra[src]


def local_attention(q_half, kv, pref, seq_count, nc, prev=None):
    slots, kh, tree_len, cols = q_half.shape
    positions = kv.shape[1]
    groups = (cols - 2 * HEAD_WIDTH) // HEAD_WIDTH
    kvh = kh * nc
    rows = tree_len * groups
    per_slot = seq_count // slots
    sub = rows // per_slot
    kern = functools.partial(
        attn_kernel, n_blk=positions // BLK, scale=HEAD_WIDTH ** (-0.5), groups=groups
    )
    in_specs = [
        pl.BlockSpec((None, None, tree_len, groups * HEAD_WIDTH), lambda i, k, lv: (i, k, 0, 0)),
        pl.BlockSpec((None, positions, 2 * HEAD_WIDTH), lambda i, k, lv: (i, 0, k * nc + lv[slots])),
    ]
    operands = [pref, q_half, kv]
    aliases = {}
    if prev is not None:
        in_specs += [pl.BlockSpec(memory_space=pl.ANY)] * 3
        operands += list(prev)
        aliases = {3: 0, 4: 1, 5: 2}
    grid_spec = pltpu.PrefetchScalarGridSpec(
        num_scalar_prefetch=1,
        grid=(slots, kh),
        in_specs=in_specs,
        out_specs=[
            pl.BlockSpec((None, None, 8, rows), lambda i, k, lv: (i, lv[slots] * kh + k, 0, 0)),
            pl.BlockSpec((None, None, 8, rows), lambda i, k, lv: (i, lv[slots] * kh + k, 0, 0)),
            pl.BlockSpec(
                (per_slot, None, sub, HEAD_WIDTH), lambda i, k, lv: (i, lv[slots] * kh + k, 0, 0)
            ),
        ],
    )
    return pl.pallas_call(
        kern,
        grid_spec=grid_spec,
        out_shape=[
            jax.ShapeDtypeStruct((slots, kvh, 8, rows), jnp.float32),
            jax.ShapeDtypeStruct((slots, kvh, 8, rows), jnp.float32),
            jax.ShapeDtypeStruct((seq_count, kvh, sub, HEAD_WIDTH), jnp.float32),
        ],
        input_output_aliases=aliases,
        compiler_params=pltpu.CompilerParams(
            dimension_semantics=("arbitrary", "arbitrary"),
            vmem_limit_bytes=48 * 1024 * 1024,
        ),
    )(*operands)


def merge_pair(m, l, acc, axis):
    top = jnp.max(m, axis=axis, keepdims=True)
    f = jnp.exp(m - top)
    return (
        jnp.squeeze(top, axis),
        jnp.sum(f * l, axis=axis),
        jnp.sum(f[..., None] * acc, axis=axis),
    )


def body(queries, draft_key_value, kv_cache, cache_lengths, ancestors, dealing, accepted_path):
    local_reqs = kv_cache.shape[0]
    tree_len = queries.shape[1]
    picker = (
        accepted_path[:, :, None] == jnp.arange(tree_len, dtype=jnp.int32)[None, None, :]
    ).astype(jnp.bfloat16)
    kept_entries = jnp.einsum(
        "rit,rtc->ric", picker, draft_key_value, preferred_element_type=jnp.float32
    ).astype(jnp.bfloat16)

    nz, ny, nx, nc = (lax.axis_size(a) for a in ("z", "y", "x", "c"))
    zi, yi, xi, ci = (lax.axis_index(a) for a in ("z", "y", "x", "c"))
    seq_count = nx * nc
    position = xi * nc + ci
    q_cols = queries.shape[2]
    d_cols = draft_key_value.shape[2]

    both = jnp.concatenate([queries, draft_key_value], axis=2)
    held = lax.all_gather(both, "z", axis=0, tiled=True)
    dest_slot = jnp.arange(ny * local_reqs, dtype=jnp.int32) + (zi * ny) * local_reqs
    wanted = dealing[dest_slot]
    src_group = wanted // local_reqs
    pick = (src_group // ny) * local_reqs + wanted % local_reqs
    send = jnp.take(held, pick, axis=0).reshape((ny, local_reqs) + both.shape[1:])
    recv = lax.all_to_all(send, "y", 0, 0, tiled=True)
    my_group = zi * ny + yi
    mine = lax.dynamic_slice_in_dim(dealing, my_group * local_reqs, local_reqs)
    from_y = (mine // local_reqs) % ny
    recv = recv.reshape((ny * local_reqs,) + both.shape[1:])
    own = jnp.take(recv, from_y * local_reqs + jnp.arange(local_reqs, dtype=jnp.int32), axis=0)

    own_x = lax.all_gather(own, "x", axis=1, tiled=False)
    other_x = lax.ppermute(own_x, "c", perm=[(0, 1), (1, 0)])

    positions = kv_cache.shape[1]
    kv_heads = kv_cache.shape[2] // (2 * HEAD_WIDTH)
    groups = q_cols // HEAD_WIDTH
    live = jnp.clip(cache_lengths - position * positions, 0, positions).astype(jnp.int32)
    first_out = local_attention(own_x, kv_cache, jnp.concatenate([live, ci[None]]), seq_count, nc)
    m_rows, l_rows, part_acc = local_attention(
        other_x, kv_cache, jnp.concatenate([live, (1 - ci)[None]]), seq_count, nc, prev=first_out
    )
    first = ci == 0
    per_slot = seq_count // local_reqs
    tok = tree_len // per_slot

    def dest_major(rows_arr):
        r = rows_arr[:, :, 0, :].reshape(local_reqs, kv_heads, groups, per_slot, tok)
        return r.transpose(0, 3, 1, 2, 4).reshape(seq_count, kv_heads, groups * tok)

    part_m = dest_major(m_rows)
    part_l = dest_major(l_rows)
    sub = part_acc.shape[2]
    rows_acc = kv_heads * sub
    stat_rows = rows_acc // HEAD_WIDTH
    pad = (-(rows_acc + 2 * stat_rows)) % 8

    def pack(acc, m, l):
        lead = acc.shape[:-2]
        parts = [acc, m.reshape(lead + (stat_rows, HEAD_WIDTH)), l.reshape(lead + (stat_rows, HEAD_WIDTH))]
        if pad:
            parts.append(jnp.zeros(lead + (pad, HEAD_WIDTH), jnp.float32))
        return jnp.concatenate(parts, axis=-2)

    def unpack(pk):
        lead = pk.shape[:-2]
        acc = pk[..., :rows_acc, :]
        m = pk[..., rows_acc:rows_acc + stat_rows, :].reshape(lead + (rows_acc,))
        l = pk[..., rows_acc + stat_rows:rows_acc + 2 * stat_rows, :].reshape(lead + (rows_acc,))
        return m, l, acc

    pk = pack(
        part_acc.reshape(nx, nc, rows_acc, HEAD_WIDTH),
        part_m.reshape(nx, nc, rows_acc),
        part_l.reshape(nx, nc, rows_acc),
    )
    pk = lax.all_to_all(pk, "c", 1, 1, tiled=True)
    m1, l1, a1 = merge_pair(*unpack(pk), axis=1)
    pk = lax.all_to_all(pack(a1, m1, l1), "x", 0, 0, tiled=True)
    rm, rl, acc = unpack(pk)

    my_slot = position // per_slot
    my_tok0 = (position % per_slot) * tok
    mine_own = lax.dynamic_index_in_dim(own_x, my_slot, 0, keepdims=False)
    mine_other = lax.dynamic_index_in_dim(other_x, my_slot, 0, keepdims=False)
    mine_all = jnp.where(
        first,
        jnp.concatenate([mine_own, mine_other], axis=0),
        jnp.concatenate([mine_other, mine_own], axis=0),
    )
    q_mine = lax.dynamic_slice_in_dim(mine_all[..., :q_cols], my_tok0, tok, 1).reshape(
        kv_heads, tok, groups, HEAD_WIDTH
    )
    d_slot = mine_all[..., q_cols:].reshape(kv_heads, tree_len, 2, HEAD_WIDTH)
    anc = lax.dynamic_index_in_dim(ancestors, my_slot, 0, keepdims=False)
    anc = lax.dynamic_slice_in_dim(anc, my_tok0, tok, 0)
    allowed = (anc > 0)[None, None, :, :]
    sd = jnp.einsum(
        "ktgd,kjd->kgtj", q_mine, d_slot[:, :, 0], preferred_element_type=jnp.float32
    ) * HEAD_WIDTH ** (-0.5)
    sd = jnp.where(allowed, sd, jnp.float32(NEG))
    md = jnp.max(sd, axis=-1)
    wd = jnp.where(allowed, jnp.exp(sd - md[..., None]), jnp.float32(0.0))
    ld = jnp.sum(wd, axis=-1)
    od = jnp.einsum(
        "kgtj,kjd->kgtd", wd.astype(jnp.bfloat16), d_slot[:, :, 1], preferred_element_type=jnp.float32
    )
    md = md.reshape(1, kv_heads * sub)
    ld = ld.reshape(1, kv_heads * sub)
    od = od.reshape(1, kv_heads * sub, HEAD_WIDTH)

    _, den, num = merge_pair(
        jnp.concatenate([rm, md], axis=0),
        jnp.concatenate([rl, ld], axis=0),
        jnp.concatenate([acc, od], axis=0),
        axis=0,
    )
    res = num / den[..., None]
    context = (
        res.reshape(nc, kv_heads // nc, groups, tok, HEAD_WIDTH)
        .transpose(3, 1, 0, 2, 4)
        .reshape(tok, kv_heads * groups * HEAD_WIDTH)
        .astype(jnp.bfloat16)
    )
    return (context, kept_entries)


def solution(mesh):
    req, seq = mesh.shape["req"], mesh.shape["seq"]
    nc = 2
    nx = seq // nc
    ny = int(round(req ** 0.5))
    nz = req // ny
    fine = jax.sharding.Mesh(mesh.devices.reshape(nz, ny, nx, nc), ("z", "y", "x", "c"))
    R, S = ("z", "y"), ("x", "c")
    placed = (
        P(R, None, S),
        P(R, None, S),
        P(R, S, None),
        P(R),
        P(R, None, None),
        P(),
        P(R, None),
    )
    return jax.shard_map(
        body,
        mesh=fine,
        in_specs=placed,
        out_specs=(P(R + S, None), P(R, None, S)),
        check_vma=False,
    )
```

```python
import functools

import jax
import jax.numpy as jnp
from jax import lax
from jax.experimental import pallas as pl
from jax.experimental.pallas import tpu as pltpu
from jax.sharding import PartitionSpec as P

HEAD_WIDTH = 128
BLK = 1024
NEG = -1e30


def attn_kernel(live_ref, q_ref, kv_ref, *refs, n_blk, scale, groups):
    m_ref, l_ref, acc_ref = refs[-3:]
    slot = pl.program_id(0)
    live = live_ref[slot]
    tree_len = q_ref.shape[0]
    rows = tree_len * groups
    q = jnp.concatenate(
        [q_ref[:, g * HEAD_WIDTH:(g + 1) * HEAD_WIDTH] for g in range(groups)], axis=0
    )
    run = None
    for b in range(n_blk):
        keys = kv_ref[b * BLK:(b + 1) * BLK, 0:HEAD_WIDTH]
        vals = kv_ref[b * BLK:(b + 1) * BLK, HEAD_WIDTH:2 * HEAD_WIDTH]
        s = lax.dot_general(
            q, keys, (((1,), (1,)), ((), ())), preferred_element_type=jnp.float32
        ) * scale
        pos = b * BLK + lax.broadcasted_iota(jnp.int32, (1, BLK), 1)
        allowed = pos < live
        s = jnp.where(allowed, s, jnp.float32(NEG))
        mb = jnp.max(s, axis=1, keepdims=True)
        w = jnp.exp(s - jnp.where(live > b * BLK, mb, jnp.float32(0.0)))
        lb = jnp.sum(w, axis=1, keepdims=True)
        ob = jnp.dot(w.astype(jnp.bfloat16), vals, preferred_element_type=jnp.float32)
        if run is None:
            run = (mb, lb, ob)
        else:
            rm, rl, ra = run
            nm = jnp.maximum(rm, mb)
            fa = jnp.exp(rm - nm)
            fb = jnp.exp(mb - nm)
            run = (nm, rl * fa + lb * fb, ra * fa + ob * fb)
    rm, rl, ra = run
    m_ref[...] = jnp.transpose(jnp.broadcast_to(rm, (rows, HEAD_WIDTH)))[0:8]
    l_ref[...] = jnp.transpose(jnp.broadcast_to(rl, (rows, HEAD_WIDTH)))[0:8]
    parts = acc_ref.shape[0]
    tok = tree_len // parts
    for j in range(parts):
        for g in range(groups):
            src = slice(g * tree_len + j * tok, g * tree_len + (j + 1) * tok)
            acc_ref[j, g * tok:(g + 1) * tok, :] = ra[src]


def local_attention(q_half, kv, pref, seq_count, nc, prev=None):
    slots, kh, tree_len, cols = q_half.shape
    positions = kv.shape[1]
    groups = (cols - 2 * HEAD_WIDTH) // HEAD_WIDTH
    kvh = kh * nc
    rows = tree_len * groups
    per_slot = seq_count // slots
    sub = rows // per_slot
    kern = functools.partial(
        attn_kernel, n_blk=positions // BLK, scale=HEAD_WIDTH ** (-0.5), groups=groups
    )
    in_specs = [
        pl.BlockSpec((None, None, tree_len, groups * HEAD_WIDTH), lambda i, k, lv: (i, k, 0, 0)),
        pl.BlockSpec((None, positions, 2 * HEAD_WIDTH), lambda i, k, lv: (i, 0, k * nc + lv[slots])),
    ]
    operands = [pref, q_half, kv]
    aliases = {}
    if prev is not None:
        in_specs += [pl.BlockSpec(memory_space=pl.ANY)] * 3
        operands += list(prev)
        aliases = {3: 0, 4: 1, 5: 2}
    grid_spec = pltpu.PrefetchScalarGridSpec(
        num_scalar_prefetch=1,
        grid=(slots, kh),
        in_specs=in_specs,
        out_specs=[
            pl.BlockSpec((None, None, 8, rows), lambda i, k, lv: (i, lv[slots] * kh + k, 0, 0)),
            pl.BlockSpec((None, None, 8, rows), lambda i, k, lv: (i, lv[slots] * kh + k, 0, 0)),
            pl.BlockSpec(
                (per_slot, None, sub, HEAD_WIDTH), lambda i, k, lv: (i, lv[slots] * kh + k, 0, 0)
            ),
        ],
    )
    return pl.pallas_call(
        kern,
        grid_spec=grid_spec,
        out_shape=[
            jax.ShapeDtypeStruct((slots, kvh, 8, rows), jnp.float32),
            jax.ShapeDtypeStruct((slots, kvh, 8, rows), jnp.float32),
            jax.ShapeDtypeStruct((seq_count, kvh, sub, HEAD_WIDTH), jnp.float32),
        ],
        input_output_aliases=aliases,
        compiler_params=pltpu.CompilerParams(
            dimension_semantics=("arbitrary", "arbitrary"),
            vmem_limit_bytes=48 * 1024 * 1024,
        ),
    )(*operands)


def merge_pair(m, l, acc, axis):
    top = jnp.max(m, axis=axis, keepdims=True)
    f = jnp.exp(m - top)
    return (
        jnp.squeeze(top, axis),
        jnp.sum(f * l, axis=axis),
        jnp.sum(f[..., None] * acc, axis=axis),
    )


def body(queries, draft_key_value, kv_cache, cache_lengths, ancestors, dealing, accepted_path):
    local_reqs = kv_cache.shape[0]
    tree_len = queries.shape[1]
    picker = (
        accepted_path[:, :, None] == jnp.arange(tree_len, dtype=jnp.int32)[None, None, :]
    ).astype(jnp.bfloat16)
    kept_entries = jnp.einsum(
        "rit,rtc->ric", picker, draft_key_value, preferred_element_type=jnp.float32
    ).astype(jnp.bfloat16)

    nz, ny, nx, nc = (lax.axis_size(a) for a in ("z", "y", "x", "c"))
    zi, yi, xi, ci = (lax.axis_index(a) for a in ("z", "y", "x", "c"))
    seq_count = nx * nc
    position = xi * nc + ci
    q_cols = queries.shape[2]
    d_cols = draft_key_value.shape[2]

    both = jnp.concatenate([queries, draft_key_value], axis=2)
    held = lax.all_gather(both, "z", axis=0, tiled=True)
    dest_slot = jnp.arange(ny * local_reqs, dtype=jnp.int32) + (zi * ny) * local_reqs
    wanted = dealing[dest_slot]
    src_group = wanted // local_reqs
    pick = (src_group // ny) * local_reqs + wanted % local_reqs
    send = jnp.take(held, pick, axis=0).reshape((ny, local_reqs) + both.shape[1:])
    recv = lax.all_to_all(send, "y", 0, 0, tiled=True)
    my_group = zi * ny + yi
    mine = lax.dynamic_slice_in_dim(dealing, my_group * local_reqs, local_reqs)
    from_y = (mine // local_reqs) % ny
    recv = recv.reshape((ny * local_reqs,) + both.shape[1:])
    own = jnp.take(recv, from_y * local_reqs + jnp.arange(local_reqs, dtype=jnp.int32), axis=0)

    own_x = lax.all_gather(own, "x", axis=1, tiled=False)
    other_x = lax.ppermute(own_x, "c", perm=[(0, 1), (1, 0)])

    positions = kv_cache.shape[1]
    kv_heads = kv_cache.shape[2] // (2 * HEAD_WIDTH)
    groups = q_cols // HEAD_WIDTH
    live = jnp.clip(cache_lengths - position * positions, 0, positions).astype(jnp.int32)
    first_out = local_attention(own_x, kv_cache, jnp.concatenate([live, ci[None]]), seq_count, nc)
    m_rows, l_rows, part_acc = local_attention(
        other_x, kv_cache, jnp.concatenate([live, (1 - ci)[None]]), seq_count, nc, prev=first_out
    )
    first = ci == 0
    per_slot = seq_count // local_reqs
    tok = tree_len // per_slot

    def dest_major(rows_arr):
        r = rows_arr[:, :, 0, :].reshape(local_reqs, kv_heads, groups, per_slot, tok)
        return r.transpose(0, 3, 1, 2, 4).reshape(seq_count, kv_heads, groups * tok)

    part_m = dest_major(m_rows)
    part_l = dest_major(l_rows)
    sub = part_acc.shape[2]
    rows_acc = kv_heads * sub
    stat_rows = rows_acc // HEAD_WIDTH
    pad = (-(rows_acc + 2 * stat_rows)) % 8

    def pack(acc, m, l):
        lead = acc.shape[:-2]
        parts = [acc, m.reshape(lead + (stat_rows, HEAD_WIDTH)), l.reshape(lead + (stat_rows, HEAD_WIDTH))]
        if pad:
            parts.append(jnp.zeros(lead + (pad, HEAD_WIDTH), jnp.float32))
        return jnp.concatenate(parts, axis=-2)

    def unpack(pk):
        lead = pk.shape[:-2]
        acc = pk[..., :rows_acc, :]
        m = pk[..., rows_acc:rows_acc + stat_rows, :].reshape(lead + (rows_acc,))
        l = pk[..., rows_acc + stat_rows:rows_acc + 2 * stat_rows, :].reshape(lead + (rows_acc,))
        return m, l, acc

    pk = pack(
        part_acc.reshape(nx, nc, rows_acc, HEAD_WIDTH),
        part_m.reshape(nx, nc, rows_acc),
        part_l.reshape(nx, nc, rows_acc),
    )
    pk = lax.all_to_all(pk, "c", 1, 1, tiled=True)
    m1, l1, a1 = merge_pair(*unpack(pk), axis=1)
    pk = lax.all_to_all(pack(a1, m1, l1), "x", 0, 0, tiled=True)
    rm, rl, acc = unpack(pk)

    my_slot = position // per_slot
    my_tok0 = (position % per_slot) * tok
    mine_own = lax.dynamic_index_in_dim(own_x, my_slot, 0, keepdims=False)
    mine_other = lax.dynamic_index_in_dim(other_x, my_slot, 0, keepdims=False)
    mine_all = jnp.where(
        first,
        jnp.concatenate([mine_own, mine_other], axis=0),
        jnp.concatenate([mine_other, mine_own], axis=0),
    )
    q_mine = lax.dynamic_slice_in_dim(mine_all[..., :q_cols], my_tok0, tok, 1).reshape(
        kv_heads, tok, groups, HEAD_WIDTH
    )
    d_slot = mine_all[..., q_cols:].reshape(kv_heads, tree_len, 2, HEAD_WIDTH)
    anc = lax.dynamic_index_in_dim(ancestors, my_slot, 0, keepdims=False)
    anc = lax.dynamic_slice_in_dim(anc, my_tok0, tok, 0)
    allowed = (anc > 0)[None, None, :, :]
    sd = jnp.einsum(
        "ktgd,kjd->kgtj", q_mine, d_slot[:, :, 0], preferred_element_type=jnp.float32
    ) * HEAD_WIDTH ** (-0.5)
    sd = jnp.where(allowed, sd, jnp.float32(NEG))
    md = jnp.max(sd, axis=-1)
    wd = jnp.where(allowed, jnp.exp(sd - md[..., None]), jnp.float32(0.0))
    ld = jnp.sum(wd, axis=-1)
    od = jnp.einsum(
        "kgtj,kjd->kgtd", wd.astype(jnp.bfloat16), d_slot[:, :, 1], preferred_element_type=jnp.float32
    )
    md = md.reshape(1, kv_heads * sub)
    ld = ld.reshape(1, kv_heads * sub)
    od = od.reshape(1, kv_heads * sub, HEAD_WIDTH)

    _, den, num = merge_pair(
        jnp.concatenate([rm, md], axis=0),
        jnp.concatenate([rl, ld], axis=0),
        jnp.concatenate([acc, od], axis=0),
        axis=0,
    )
    res = num / den[..., None]
    context = (
        res.reshape(nc, kv_heads // nc, groups, tok, HEAD_WIDTH)
        .transpose(3, 1, 0, 2, 4)
        .reshape(tok, kv_heads * groups * HEAD_WIDTH)
        .astype(jnp.bfloat16)
    )
    return (context, kept_entries)


def solution(mesh):
    req, seq = mesh.shape["req"], mesh.shape["seq"]
    nc = 2
    nx = seq // nc
    ny = int(round(req ** 0.5))
    nz = req // ny
    fine = jax.sharding.Mesh(mesh.devices.reshape(nz, ny, nx, nc), ("z", "y", "x", "c"))
    R, S = ("z", "y"), ("x", "c")
    placed = (
        P(R, None, S),
        P(R, None, S),
        P(R, S, None),
        P(R),
        P(R, None, None),
        P(),
        P(R, None),
    )
    return jax.shard_map(
        body,
        mesh=fine,
        in_specs=placed,
        out_specs=(P(R + S, None), P(R, None, S)),
        check_vma=False,
    )
```

```python
import functools

import jax
import jax.numpy as jnp
from jax import lax
from jax.experimental import pallas as pl
from jax.experimental.pallas import tpu as pltpu
from jax.sharding import PartitionSpec as P

HEAD_WIDTH = 128
BLK = 1024
NEG = -1e30


def attn_kernel(live_ref, q_ref, kv_ref, *refs, n_blk, scale, groups):
    m_ref, l_ref, acc_ref = refs[-3:]
    slot = pl.program_id(0)
    live = live_ref[slot]
    tree_len = q_ref.shape[0]
    rows = tree_len * groups
    q = jnp.concatenate(
        [q_ref[:, g * HEAD_WIDTH:(g + 1) * HEAD_WIDTH] for g in range(groups)], axis=0
    )
    run = None
    for b in range(n_blk):
        keys = kv_ref[b * BLK:(b + 1) * BLK, 0:HEAD_WIDTH]
        vals = kv_ref[b * BLK:(b + 1) * BLK, HEAD_WIDTH:2 * HEAD_WIDTH]
        s = lax.dot_general(
            q, keys, (((1,), (1,)), ((), ())), preferred_element_type=jnp.float32
        ) * scale
        pos = b * BLK + lax.broadcasted_iota(jnp.int32, (1, BLK), 1)
        allowed = pos < live
        s = jnp.where(allowed, s, jnp.float32(NEG))
        mb = jnp.max(s, axis=1, keepdims=True)
        w = jnp.exp(s - jnp.where(live > b * BLK, mb, jnp.float32(0.0)))
        lb = jnp.sum(w, axis=1, keepdims=True)
        ob = jnp.dot(w.astype(jnp.bfloat16), vals, preferred_element_type=jnp.float32)
        if run is None:
            run = (mb, lb, ob)
        else:
            rm, rl, ra = run
            nm = jnp.maximum(rm, mb)
            fa = jnp.exp(rm - nm)
            fb = jnp.exp(mb - nm)
            run = (nm, rl * fa + lb * fb, ra * fa + ob * fb)
    rm, rl, ra = run
    m_ref[...] = jnp.transpose(jnp.broadcast_to(rm, (rows, HEAD_WIDTH)))[0:8]
    l_ref[...] = jnp.transpose(jnp.broadcast_to(rl, (rows, HEAD_WIDTH)))[0:8]
    parts = acc_ref.shape[0]
    tok = tree_len // parts
    for j in range(parts):
        for g in range(groups):
            src = slice(g * tree_len + j * tok, g * tree_len + (j + 1) * tok)
            acc_ref[j, g * tok:(g + 1) * tok, :] = ra[src]


def local_attention(q_half, kv, pref, seq_count, nc, prev=None):
    slots, kh, tree_len, cols = q_half.shape
    positions = kv.shape[1]
    groups = (cols - 2 * HEAD_WIDTH) // HEAD_WIDTH
    kvh = kh * nc
    rows = tree_len * groups
    per_slot = seq_count // slots
    sub = rows // per_slot
    kern = functools.partial(
        attn_kernel, n_blk=positions // BLK, scale=HEAD_WIDTH ** (-0.5), groups=groups
    )
    in_specs = [
        pl.BlockSpec((None, None, tree_len, groups * HEAD_WIDTH), lambda i, k, lv: (i, k, 0, 0)),
        pl.BlockSpec((None, positions, 2 * HEAD_WIDTH), lambda i, k, lv: (i, 0, k * nc + lv[slots])),
    ]
    operands = [pref, q_half, kv]
    aliases = {}
    if prev is not None:
        in_specs += [pl.BlockSpec(memory_space=pl.ANY)] * 3
        operands += list(prev)
        aliases = {3: 0, 4: 1, 5: 2}
    grid_spec = pltpu.PrefetchScalarGridSpec(
        num_scalar_prefetch=1,
        grid=(slots, kh),
        in_specs=in_specs,
        out_specs=[
            pl.BlockSpec((None, None, 8, rows), lambda i, k, lv: (i, lv[slots] * kh + k, 0, 0)),
            pl.BlockSpec((None, None, 8, rows), lambda i, k, lv: (i, lv[slots] * kh + k, 0, 0)),
            pl.BlockSpec(
                (per_slot, None, sub, HEAD_WIDTH), lambda i, k, lv: (i, lv[slots] * kh + k, 0, 0)
            ),
        ],
    )
    return pl.pallas_call(
        kern,
        grid_spec=grid_spec,
        out_shape=[
            jax.ShapeDtypeStruct((slots, kvh, 8, rows), jnp.float32),
            jax.ShapeDtypeStruct((slots, kvh, 8, rows), jnp.float32),
            jax.ShapeDtypeStruct((seq_count, kvh, sub, HEAD_WIDTH), jnp.float32),
        ],
        input_output_aliases=aliases,
        compiler_params=pltpu.CompilerParams(
            dimension_semantics=("arbitrary", "arbitrary"),
            vmem_limit_bytes=48 * 1024 * 1024,
        ),
    )(*operands)


def merge_pair(m, l, acc, axis):
    top = jnp.max(m, axis=axis, keepdims=True)
    f = jnp.exp(m - top)
    return (
        jnp.squeeze(top, axis),
        jnp.sum(f * l, axis=axis),
        jnp.sum(f[..., None] * acc, axis=axis),
    )


def body(queries, draft_key_value, kv_cache, cache_lengths, ancestors, dealing, accepted_path):
    local_reqs = kv_cache.shape[0]
    tree_len = queries.shape[1]
    picker = (
        accepted_path[:, :, None] == jnp.arange(tree_len, dtype=jnp.int32)[None, None, :]
    ).astype(jnp.bfloat16)
    kept_entries = jnp.einsum(
        "rit,rtc->ric", picker, draft_key_value, preferred_element_type=jnp.float32
    ).astype(jnp.bfloat16)

    nz, ny, nx, nc = (lax.axis_size(a) for a in ("z", "y", "x", "c"))
    zi, yi, xi, ci = (lax.axis_index(a) for a in ("z", "y", "x", "c"))
    seq_count = nx * nc
    position = xi * nc + ci
    q_cols = queries.shape[2]
    d_cols = draft_key_value.shape[2]

    both = jnp.concatenate([queries, draft_key_value], axis=2)
    held = lax.all_gather(both, "z", axis=0, tiled=True)
    dest_slot = jnp.arange(ny * local_reqs, dtype=jnp.int32) + (zi * ny) * local_reqs
    wanted = dealing[dest_slot]
    src_group = wanted // local_reqs
    pick = (src_group // ny) * local_reqs + wanted % local_reqs
    send = jnp.take(held, pick, axis=0).reshape((ny, local_reqs) + both.shape[1:])
    recv = lax.all_to_all(send, "y", 0, 0, tiled=True)
    my_group = zi * ny + yi
    mine = lax.dynamic_slice_in_dim(dealing, my_group * local_reqs, local_reqs)
    from_y = (mine // local_reqs) % ny
    recv = recv.reshape((ny * local_reqs,) + both.shape[1:])
    own = jnp.take(recv, from_y * local_reqs + jnp.arange(local_reqs, dtype=jnp.int32), axis=0)

    own_x = lax.all_gather(own, "x", axis=1, tiled=False)
    other_x = lax.ppermute(own_x, "c", perm=[(0, 1), (1, 0)])

    positions = kv_cache.shape[1]
    kv_heads = kv_cache.shape[2] // (2 * HEAD_WIDTH)
    groups = q_cols // HEAD_WIDTH
    live = jnp.clip(cache_lengths - position * positions, 0, positions).astype(jnp.int32)
    first_out = local_attention(own_x, kv_cache, jnp.concatenate([live, ci[None]]), seq_count, nc)
    m_rows, l_rows, part_acc = local_attention(
        other_x, kv_cache, jnp.concatenate([live, (1 - ci)[None]]), seq_count, nc, prev=first_out
    )
    first = ci == 0
    per_slot = seq_count // local_reqs
    tok = tree_len // per_slot

    def dest_major(rows_arr):
        r = rows_arr[:, :, 0, :].reshape(local_reqs, kv_heads, groups, per_slot, tok)
        return r.transpose(0, 3, 1, 2, 4).reshape(seq_count, kv_heads, groups * tok)

    part_m = dest_major(m_rows)
    part_l = dest_major(l_rows)
    sub = part_acc.shape[2]
    rows_acc = kv_heads * sub
    stat_rows = rows_acc // HEAD_WIDTH
    pad = (-(rows_acc + 2 * stat_rows)) % 8

    def pack(acc, m, l):
        lead = acc.shape[:-2]
        parts = [acc, m.reshape(lead + (stat_rows, HEAD_WIDTH)), l.reshape(lead + (stat_rows, HEAD_WIDTH))]
        if pad:
            parts.append(jnp.zeros(lead + (pad, HEAD_WIDTH), jnp.float32))
        return jnp.concatenate(parts, axis=-2)

    def unpack(pk):
        lead = pk.shape[:-2]
        acc = pk[..., :rows_acc, :]
        m = pk[..., rows_acc:rows_acc + stat_rows, :].reshape(lead + (rows_acc,))
        l = pk[..., rows_acc + stat_rows:rows_acc + 2 * stat_rows, :].reshape(lead + (rows_acc,))
        return m, l, acc

    pk = pack(
        part_acc.reshape(nx, nc, rows_acc, HEAD_WIDTH),
        part_m.reshape(nx, nc, rows_acc),
        part_l.reshape(nx, nc, rows_acc),
    )
    pk = lax.all_to_all(pk, "c", 1, 1, tiled=True)
    m1, l1, a1 = merge_pair(*unpack(pk), axis=1)
    pk = lax.all_to_all(pack(a1, m1, l1), "x", 0, 0, tiled=True)
    rm, rl, acc = unpack(pk)

    my_slot = position // per_slot
    my_tok0 = (position % per_slot) * tok
    late_own, late_other, _ = lax.optimization_barrier((own_x, other_x, part_acc))
    mine_own = lax.dynamic_index_in_dim(late_own, my_slot, 0, keepdims=False)
    mine_other = lax.dynamic_index_in_dim(late_other, my_slot, 0, keepdims=False)
    mine_all = jnp.where(
        first,
        jnp.concatenate([mine_own, mine_other], axis=0),
        jnp.concatenate([mine_other, mine_own], axis=0),
    )
    q_mine = lax.dynamic_slice_in_dim(mine_all[..., :q_cols], my_tok0, tok, 1).reshape(
        kv_heads, tok, groups, HEAD_WIDTH
    )
    d_slot = mine_all[..., q_cols:].reshape(kv_heads, tree_len, 2, HEAD_WIDTH)
    anc = lax.dynamic_index_in_dim(ancestors, my_slot, 0, keepdims=False)
    anc = lax.dynamic_slice_in_dim(anc, my_tok0, tok, 0)
    allowed = (anc > 0)[None, None, :, :]
    sd = jnp.einsum(
        "ktgd,kjd->kgtj", q_mine, d_slot[:, :, 0], preferred_element_type=jnp.float32
    ) * HEAD_WIDTH ** (-0.5)
    sd = jnp.where(allowed, sd, jnp.float32(NEG))
    md = jnp.max(sd, axis=-1)
    wd = jnp.where(allowed, jnp.exp(sd - md[..., None]), jnp.float32(0.0))
    ld = jnp.sum(wd, axis=-1)
    od = jnp.einsum(
        "kgtj,kjd->kgtd", wd.astype(jnp.bfloat16), d_slot[:, :, 1], preferred_element_type=jnp.float32
    )
    md = md.reshape(1, kv_heads * sub)
    ld = ld.reshape(1, kv_heads * sub)
    od = od.reshape(1, kv_heads * sub, HEAD_WIDTH)

    _, den, num = merge_pair(
        jnp.concatenate([rm, md], axis=0),
        jnp.concatenate([rl, ld], axis=0),
        jnp.concatenate([acc, od], axis=0),
        axis=0,
    )
    res = num / den[..., None]
    context = (
        res.reshape(nc, kv_heads // nc, groups, tok, HEAD_WIDTH)
        .transpose(3, 1, 0, 2, 4)
        .reshape(tok, kv_heads * groups * HEAD_WIDTH)
        .astype(jnp.bfloat16)
    )
    return (context, kept_entries)


def solution(mesh):
    req, seq = mesh.shape["req"], mesh.shape["seq"]
    nc = 2
    nx = seq // nc
    ny = int(round(req ** 0.5))
    nz = req // ny
    fine = jax.sharding.Mesh(mesh.devices.reshape(nz, ny, nx, nc), ("z", "y", "x", "c"))
    R, S = ("z", "y"), ("x", "c")
    placed = (
        P(R, None, S),
        P(R, None, S),
        P(R, S, None),
        P(R),
        P(R, None, None),
        P(),
        P(R, None),
    )
    return jax.shard_map(
        body,
        mesh=fine,
        in_specs=placed,
        out_specs=(P(R + S, None), P(R, None, S)),
        check_vma=False,
    )
```

```python
import functools

import jax
import jax.numpy as jnp
from jax import lax
from jax.experimental import pallas as pl
from jax.experimental.pallas import tpu as pltpu
from jax.sharding import PartitionSpec as P

HEAD_WIDTH = 128
BLK = 1024
NEG = -1e30


def attn_kernel(live_ref, q_ref, kv_ref, *refs, n_blk, scale, groups):
    m_ref, l_ref, acc_ref = refs[-3:]
    slot = pl.program_id(0)
    live = live_ref[slot]
    tree_len = q_ref.shape[0]
    rows = tree_len * groups
    q = jnp.concatenate(
        [q_ref[:, g * HEAD_WIDTH:(g + 1) * HEAD_WIDTH] for g in range(groups)], axis=0
    )
    run = None
    for b in range(n_blk):
        keys = kv_ref[b * BLK:(b + 1) * BLK, 0:HEAD_WIDTH]
        vals = kv_ref[b * BLK:(b + 1) * BLK, HEAD_WIDTH:2 * HEAD_WIDTH]
        s = lax.dot_general(
            q, keys, (((1,), (1,)), ((), ())), preferred_element_type=jnp.float32
        ) * scale
        pos = b * BLK + lax.broadcasted_iota(jnp.int32, (1, BLK), 1)
        allowed = pos < live
        s = jnp.where(allowed, s, jnp.float32(NEG))
        mb = jnp.max(s, axis=1, keepdims=True)
        w = jnp.exp(s - jnp.where(live > b * BLK, mb, jnp.float32(0.0)))
        lb = jnp.sum(w, axis=1, keepdims=True)
        ob = jnp.dot(w.astype(jnp.bfloat16), vals, preferred_element_type=jnp.float32)
        if run is None:
            run = (mb, lb, ob)
        else:
            rm, rl, ra = run
            nm = jnp.maximum(rm, mb)
            fa = jnp.exp(rm - nm)
            fb = jnp.exp(mb - nm)
            run = (nm, rl * fa + lb * fb, ra * fa + ob * fb)
    rm, rl, ra = run
    m_ref[...] = jnp.transpose(jnp.broadcast_to(rm, (rows, HEAD_WIDTH)))[0:8]
    l_ref[...] = jnp.transpose(jnp.broadcast_to(rl, (rows, HEAD_WIDTH)))[0:8]
    parts = acc_ref.shape[0]
    tok = tree_len // parts
    for j in range(parts):
        for g in range(groups):
            src = slice(g * tree_len + j * tok, g * tree_len + (j + 1) * tok)
            acc_ref[j, g * tok:(g + 1) * tok, :] = ra[src]


def local_attention(q_half, kv, pref, seq_count, nc, prev=None):
    slots, kh, tree_len, cols = q_half.shape
    positions = kv.shape[1]
    groups = (cols - 2 * HEAD_WIDTH) // HEAD_WIDTH
    kvh = kh * nc
    rows = tree_len * groups
    per_slot = seq_count // slots
    sub = rows // per_slot
    kern = functools.partial(
        attn_kernel, n_blk=positions // BLK, scale=HEAD_WIDTH ** (-0.5), groups=groups
    )
    in_specs = [
        pl.BlockSpec((None, None, tree_len, groups * HEAD_WIDTH), lambda i, k, lv: (i, k, 0, 0)),
        pl.BlockSpec((None, positions, 2 * HEAD_WIDTH), lambda i, k, lv: (i, 0, k * nc + lv[slots])),
    ]
    operands = [pref, q_half, kv]
    aliases = {}
    if prev is not None:
        in_specs += [pl.BlockSpec(memory_space=pl.ANY)] * 3
        operands += list(prev)
        aliases = {3: 0, 4: 1, 5: 2}
    grid_spec = pltpu.PrefetchScalarGridSpec(
        num_scalar_prefetch=1,
        grid=(slots, kh),
        in_specs=in_specs,
        out_specs=[
            pl.BlockSpec((None, None, 8, rows), lambda i, k, lv: (i, lv[slots] * kh + k, 0, 0)),
            pl.BlockSpec((None, None, 8, rows), lambda i, k, lv: (i, lv[slots] * kh + k, 0, 0)),
            pl.BlockSpec(
                (per_slot, None, sub, HEAD_WIDTH), lambda i, k, lv: (i, lv[slots] * kh + k, 0, 0)
            ),
        ],
    )
    return pl.pallas_call(
        kern,
        grid_spec=grid_spec,
        out_shape=[
            jax.ShapeDtypeStruct((slots, kvh, 8, rows), jnp.float32),
            jax.ShapeDtypeStruct((slots, kvh, 8, rows), jnp.float32),
            jax.ShapeDtypeStruct((seq_count, kvh, sub, HEAD_WIDTH), jnp.float32),
        ],
        input_output_aliases=aliases,
        compiler_params=pltpu.CompilerParams(
            dimension_semantics=("arbitrary", "arbitrary"),
            vmem_limit_bytes=48 * 1024 * 1024,
        ),
    )(*operands)


def merge_pair(m, l, acc, axis):
    top = jnp.max(m, axis=axis, keepdims=True)
    f = jnp.exp(m - top)
    return (
        jnp.squeeze(top, axis),
        jnp.sum(f * l, axis=axis),
        jnp.sum(f[..., None] * acc, axis=axis),
    )


def body(queries, draft_key_value, kv_cache, cache_lengths, ancestors, dealing, accepted_path):
    local_reqs = kv_cache.shape[0]
    tree_len = queries.shape[1]

    nz, ny, nx, nc = (lax.axis_size(a) for a in ("z", "y", "x", "c"))
    zi, yi, xi, ci = (lax.axis_index(a) for a in ("z", "y", "x", "c"))
    seq_count = nx * nc
    position = xi * nc + ci
    q_cols = queries.shape[2]
    d_cols = draft_key_value.shape[2]

    both = jnp.concatenate([queries, draft_key_value], axis=2)
    held = lax.all_gather(both, "z", axis=0, tiled=True)
    dest_slot = jnp.arange(ny * local_reqs, dtype=jnp.int32) + (zi * ny) * local_reqs
    wanted = dealing[dest_slot]
    src_group = wanted // local_reqs
    pick = (src_group // ny) * local_reqs + wanted % local_reqs
    send = jnp.take(held, pick, axis=0).reshape((ny, local_reqs) + both.shape[1:])
    recv = lax.all_to_all(send, "y", 0, 0, tiled=True)
    my_group = zi * ny + yi
    mine = lax.dynamic_slice_in_dim(dealing, my_group * local_reqs, local_reqs)
    from_y = (mine // local_reqs) % ny
    recv = recv.reshape((ny * local_reqs,) + both.shape[1:])
    own = jnp.take(recv, from_y * local_reqs + jnp.arange(local_reqs, dtype=jnp.int32), axis=0)

    own_x = lax.all_gather(own, "x", axis=1, tiled=False)
    other_x = lax.ppermute(own_x, "c", perm=[(0, 1), (1, 0)])

    positions = kv_cache.shape[1]
    kv_heads = kv_cache.shape[2] // (2 * HEAD_WIDTH)
    groups = q_cols // HEAD_WIDTH
    live = jnp.clip(cache_lengths - position * positions, 0, positions).astype(jnp.int32)
    first_out = local_attention(own_x, kv_cache, jnp.concatenate([live, ci[None]]), seq_count, nc)
    m_rows, l_rows, part_acc = local_attention(
        other_x, kv_cache, jnp.concatenate([live, (1 - ci)[None]]), seq_count, nc, prev=first_out
    )
    first = ci == 0
    per_slot = seq_count // local_reqs
    tok = tree_len // per_slot

    def dest_major(rows_arr):
        r = rows_arr[:, :, 0, :].reshape(local_reqs, kv_heads, groups, per_slot, tok)
        return r.transpose(0, 3, 1, 2, 4).reshape(seq_count, kv_heads, groups * tok)

    part_m = dest_major(m_rows)
    part_l = dest_major(l_rows)
    sub = part_acc.shape[2]
    rows_acc = kv_heads * sub
    stat_rows = rows_acc // HEAD_WIDTH
    pad = (-(rows_acc + 2 * stat_rows)) % 8

    def pack(acc, m, l):
        lead = acc.shape[:-2]
        parts = [acc, m.reshape(lead + (stat_rows, HEAD_WIDTH)), l.reshape(lead + (stat_rows, HEAD_WIDTH))]
        if pad:
            parts.append(jnp.zeros(lead + (pad, HEAD_WIDTH), jnp.float32))
        return jnp.concatenate(parts, axis=-2)

    def unpack(pk):
        lead = pk.shape[:-2]
        acc = pk[..., :rows_acc, :]
        m = pk[..., rows_acc:rows_acc + stat_rows, :].reshape(lead + (rows_acc,))
        l = pk[..., rows_acc + stat_rows:rows_acc + 2 * stat_rows, :].reshape(lead + (rows_acc,))
        return m, l, acc

    pk = pack(
        part_acc.reshape(nx, nc, rows_acc, HEAD_WIDTH),
        part_m.reshape(nx, nc, rows_acc),
        part_l.reshape(nx, nc, rows_acc),
    )
    pk = lax.all_to_all(pk, "c", 1, 1, tiled=True)
    m1, l1, a1 = merge_pair(*unpack(pk), axis=1)
    pk = lax.all_to_all(pack(a1, m1, l1), "x", 0, 0, tiled=True)
    rm, rl, acc = unpack(pk)

    my_slot = position // per_slot
    my_tok0 = (position % per_slot) * tok
    late_draft, late_path, _ = lax.optimization_barrier((draft_key_value, accepted_path, part_acc))
    picker = (
        late_path[:, :, None] == jnp.arange(tree_len, dtype=jnp.int32)[None, None, :]
    ).astype(jnp.bfloat16)
    kept_entries = jnp.einsum(
        "rit,rtc->ric", picker, late_draft, preferred_element_type=jnp.float32
    ).astype(jnp.bfloat16)
    late_own, late_other, _ = lax.optimization_barrier((own_x, other_x, part_acc))
    mine_own = lax.dynamic_index_in_dim(late_own, my_slot, 0, keepdims=False)
    mine_other = lax.dynamic_index_in_dim(late_other, my_slot, 0, keepdims=False)
    mine_all = jnp.where(
        first,
        jnp.concatenate([mine_own, mine_other], axis=0),
        jnp.concatenate([mine_other, mine_own], axis=0),
    )
    q_mine = lax.dynamic_slice_in_dim(mine_all[..., :q_cols], my_tok0, tok, 1).reshape(
        kv_heads, tok, groups, HEAD_WIDTH
    )
    d_slot = mine_all[..., q_cols:].reshape(kv_heads, tree_len, 2, HEAD_WIDTH)
    anc = lax.dynamic_index_in_dim(ancestors, my_slot, 0, keepdims=False)
    anc = lax.dynamic_slice_in_dim(anc, my_tok0, tok, 0)
    allowed = (anc > 0)[None, None, :, :]
    sd = jnp.einsum(
        "ktgd,kjd->kgtj", q_mine, d_slot[:, :, 0], preferred_element_type=jnp.float32
    ) * HEAD_WIDTH ** (-0.5)
    sd = jnp.where(allowed, sd, jnp.float32(NEG))
    md = jnp.max(sd, axis=-1)
    wd = jnp.where(allowed, jnp.exp(sd - md[..., None]), jnp.float32(0.0))
    ld = jnp.sum(wd, axis=-1)
    od = jnp.einsum(
        "kgtj,kjd->kgtd", wd.astype(jnp.bfloat16), d_slot[:, :, 1], preferred_element_type=jnp.float32
    )
    md = md.reshape(1, kv_heads * sub)
    ld = ld.reshape(1, kv_heads * sub)
    od = od.reshape(1, kv_heads * sub, HEAD_WIDTH)

    _, den, num = merge_pair(
        jnp.concatenate([rm, md], axis=0),
        jnp.concatenate([rl, ld], axis=0),
        jnp.concatenate([acc, od], axis=0),
        axis=0,
    )
    res = num / den[..., None]
    context = (
        res.reshape(nc, kv_heads // nc, groups, tok, HEAD_WIDTH)
        .transpose(3, 1, 0, 2, 4)
        .reshape(tok, kv_heads * groups * HEAD_WIDTH)
        .astype(jnp.bfloat16)
    )
    return (context, kept_entries)


def solution(mesh):
    req, seq = mesh.shape["req"], mesh.shape["seq"]
    nc = 2
    nx = seq // nc
    ny = int(round(req ** 0.5))
    nz = req // ny
    fine = jax.sharding.Mesh(mesh.devices.reshape(nz, ny, nx, nc), ("z", "y", "x", "c"))
    R, S = ("z", "y"), ("x", "c")
    placed = (
        P(R, None, S),
        P(R, None, S),
        P(R, S, None),
        P(R),
        P(R, None, None),
        P(),
        P(R, None),
    )
    return jax.shard_map(
        body,
        mesh=fine,
        in_specs=placed,
        out_specs=(P(R + S, None), P(R, None, S)),
        check_vma=False,
    )
```
